32 devices in a mesh: rows: 4 (over x, core), aux: 8 (over z, y).
Axes of the slice: x: 2, y: 2, z: 4, core: 2. Of those that a mesh axis runs over, the one named last changes fastest.
Arguments:
- b_rows: bfloat16 [6144, 8192], P(('rows', 'aux')), may hold values from -0.079589844 to 0.079589844
- pair_index: int32 [6144], P(('rows', 'aux')), may hold values from 0 to 6143, each once
- e_occ: float32 [512], replicated, may hold values from -3 to -0.5
- e_vir: float32 [1536], replicated, may hold values from 0.2 to 3
- occ_batch: int32 [1], replicated, may hold values from 0 to 127
- freq: float32 [1], replicated, may hold values from 0.3 to 3
Outputs:
- q_matrix: float32 [8192, 8192], P('aux', 'rows')
The draws below stay inside these ranges and needn't reach their ends.
All inputs are finite; a program needn't handle non-finite values.
Results may differ from the reference program's by a relative error of at most 0.0022.
Values may be sent and summed in bfloat16 or wider, within the bound.
No kernel may reach another device: no remote copies, remote signals or barrier semaphores. Data moves between devices by JAX's collectives and lax.ppermute only.
A program may use at most 192 MiB of HBM per device.

```python
import math
import jax
import jax.numpy as jnp
from jax import lax

NAUX = 8192
NVIR = 1536
NOCC_B = 4
NOCC = 512
NOV = 6144


def raised(drawn, own_key, source, target, shards_of, factor):
    def block_of(position):
        return (jnp.arange(drawn.shape[position]) // (drawn.shape[position] // shards_of)).reshape((-1,) + (1,) * (drawn.ndim - 1 - position))

    first = jax.random.permutation(own_key, shards_of)[block_of(target)]
    far = (block_of(target) + shards_of // 2) % shards_of
    return jnp.where((block_of(source) == first) | (block_of(source) == far), factor * drawn, drawn)


def levels(rng, extent, pieces, least, largest):
    factor_of, own = 1.0, jax.random.fold_in(rng, 6)
    for axis_at, shards_of in pieces:
        heights = jnp.exp(jax.random.uniform(jax.random.fold_in(own, axis_at), (shards_of,), jnp.float32, least / len(pieces), largest / len(pieces)))
        factor_of = factor_of * jnp.repeat(heights, extent[axis_at] // shards_of).reshape([-1 if axis == axis_at else 1 for axis in range(len(extent))])
    return factor_of


def heavy_noise(rng, shape, width, most, pieces, heavy, kind=jnp.bfloat16):
    values = width * jax.random.normal(rng, shape, jnp.float32)
    if pieces:
        values = values * levels(rng, shape, pieces, -0.22, 0.18)
    return jnp.clip(raised(values, jax.random.fold_in(rng, 3), *heavy), -most, most).astype(kind)


def setup_inputs(seed: int = 0) -> dict:
    arg_keys = jax.random.split(jax.random.key(seed), 7)
    return {
        "b_rows": heavy_noise(arg_keys[0], (NOV, NAUX), 0.0128, 0.079589844, ((0, 32),), (0, 1, 32, 2.75)),
        "pair_index": jax.random.permutation(arg_keys[1], NOV).astype(jnp.int32),
        "e_occ": jnp.clip(jax.random.uniform(arg_keys[2], (NOCC,), jnp.float32, -3.0, -0.5), -3.0, -0.5),
        "e_vir": jnp.clip(jax.random.uniform(arg_keys[3], (NVIR,), jnp.float32, 0.2, 3.0), 0.2, 3.0),
        "occ_batch": jax.random.randint(arg_keys[4], (1,), 0, NOCC // NOCC_B).astype(jnp.int32),
        "freq": jnp.clip(jnp.exp(jax.random.uniform(arg_keys[5], (1,), jnp.float32, math.log(0.3), math.log(3.0))), 0.3, 3.0),
    }


def reference(b_rows, pair_index, e_occ, e_vir, occ_batch, freq):
    occ = occ_batch[0] * NOCC_B + pair_index // NVIR
    vir = pair_index % NVIR
    delta = e_vir[vir] - e_occ[occ]
    weight = 2.0 * delta / (delta * delta + freq[0] * freq[0])
    scaled = (weight[:, None] * b_rows.astype(jnp.float32)).astype(jnp.bfloat16)
    return lax.dot_general(scaled, b_rows, (((0,), (0,)), ((), ())), preferred_element_type=jnp.float32)
```

```python
import jax
import jax.numpy as jnp
from jax import lax
from jax.sharding import Mesh, PartitionSpec as P

NVIR = 1536
NOCC_B = 4


def row_weights(pairs, e_occ, e_vir, occ_batch, freq):
    batch_start = occ_batch[0] * NOCC_B
    e_batch = lax.dynamic_slice_in_dim(e_occ, batch_start, NOCC_B, 0)
    occ = pairs // NVIR
    vir = pairs % NVIR
    occ_hit = occ[:, None] == jnp.arange(NOCC_B, dtype=jnp.int32)[None, :]
    vir_hit = vir[:, None] == jnp.arange(e_vir.shape[0], dtype=jnp.int32)[None, :]
    e_low = jnp.sum(jnp.where(occ_hit, e_batch[None, :], 0.0), axis=1)
    e_high = jnp.sum(jnp.where(vir_hit, e_vir[None, :], 0.0), axis=1)
    delta = e_high - e_low
    return 2.0 * delta / (delta * delta + freq[0] * freq[0])


def contract(left, right):
    return lax.dot_general(
        left, right, (((0,), (0,)), ((), ())), preferred_element_type=jnp.float32
    )


def make_body(n_rx, n_rc, n_az, n_ay):
    def body(b_rows, pair_index, e_occ, e_vir, occ_batch, freq):
        naux = b_rows.shape[1]
        width = naux // (n_az * n_ay)
        rw = naux // (n_rx * n_rc)
        weight = row_weights(pair_index, e_occ, e_vir, occ_batch, freq)
        weight = lax.all_gather(weight, "az", axis=0, tiled=True)
        weight = lax.all_gather(weight, "ay", axis=0, tiled=True)
        group = lax.all_gather(b_rows, "az", axis=0, tiled=True)
        group = lax.all_gather(group, "ay", axis=0, tiled=True)
        a = lax.axis_index("az") * n_ay + lax.axis_index("ay")
        own = lax.dynamic_slice_in_dim(group, a * width, width, axis=1)
        scaled = (weight[:, None] * own.astype(jnp.float32)).astype(jnp.bfloat16)
        blocks = group.reshape(group.shape[0], n_rx, n_rc, rw)
        partial_value = jnp.einsum(
            "kp,kxcr->cxpr", scaled, blocks, preferred_element_type=jnp.float32
        )
        partial_value = lax.psum_scatter(partial_value, "rc", scatter_dimension=0, tiled=True)
        partial_value = lax.psum_scatter(partial_value, "rx", scatter_dimension=1, tiled=True)
        return partial_value.reshape(width, rw)

    return body


def solution(mesh):
    n_rows = mesh.shape["rows"]
    n_aux = mesh.shape["aux"]
    n_rc = 2 if n_rows % 2 == 0 else 1
    n_ay = 2 if n_aux % 2 == 0 else 1
    n_rx = n_rows // n_rc
    n_az = n_aux // n_ay
    split = Mesh(mesh.devices.reshape(n_rx, n_rc, n_az, n_ay), ("rx", "rc", "az", "ay"))
    rows_all = ("rx", "rc", "az", "ay")
    placed = (P(rows_all, None), P(rows_all), P(), P(), P(), P())
    return jax.shard_map(
        make_body(n_rx, n_rc, n_az, n_ay),
        mesh=split,
        in_specs=placed,
        out_specs=P(("az", "ay"), ("rx", "rc")),
        check_vma=False,
    )
```

```python
import jax
import jax.numpy as jnp
from jax import lax
from jax.sharding import Mesh, PartitionSpec as P

NVIR = 1536
NOCC_B = 4
CHUNKS = 4


def row_weights(pairs, e_occ, e_vir, occ_batch, freq):
    batch_start = occ_batch[0] * NOCC_B
    e_batch = lax.dynamic_slice_in_dim(e_occ, batch_start, NOCC_B, 0)
    occ = pairs // NVIR
    vir = pairs % NVIR
    occ_hit = occ[:, None] == jnp.arange(NOCC_B, dtype=jnp.int32)[None, :]
    vir_hit = vir[:, None] == jnp.arange(e_vir.shape[0], dtype=jnp.int32)[None, :]
    e_low = jnp.sum(jnp.where(occ_hit, e_batch[None, :], 0.0), axis=1)
    e_high = jnp.sum(jnp.where(vir_hit, e_vir[None, :], 0.0), axis=1)
    delta = e_high - e_low
    return 2.0 * delta / (delta * delta + freq[0] * freq[0])


def contract(left, right):
    return lax.dot_general(
        left, right, (((0,), (0,)), ((), ())), preferred_element_type=jnp.float32
    )


def swap(x, axis):
    return lax.ppermute(x, axis, [(0, 1), (1, 0)])


def reduce_pair(parts, axis, n, dim, send_dtype):
    if n != 2:
        return lax.psum_scatter(parts, axis, scatter_dimension=dim, tiled=True)
    me = lax.axis_index(axis)
    keep = lax.dynamic_slice_in_dim(parts, me, 1, axis=dim)
    give = lax.dynamic_slice_in_dim(parts, 1 - me, 1, axis=dim)
    got = swap(give.astype(send_dtype), axis)
    return keep + got.astype(keep.dtype)


def make_body(n_rx, n_rc, n_az, n_ay):
    def body(b_rows, pair_index, e_occ, e_vir, occ_batch, freq):
        naux = b_rows.shape[1]
        width = naux // (n_az * n_ay)
        rw = naux // (n_rx * n_rc)
        chunks = CHUNKS if naux % (CHUNKS * 128) == 0 else 1
        cw = naux // chunks
        weight = row_weights(pair_index, e_occ, e_vir, occ_batch, freq)
        weight = lax.all_gather(weight, "az", axis=0, tiled=True)
        mine, theirs = [], []
        for j in range(chunks):
            piece = lax.all_gather(b_rows[:, j * cw:(j + 1) * cw], "az", axis=0, tiled=True)
            mine.append(piece)
            theirs.append(swap(piece, "ay") if n_ay == 2 else piece)
        if n_ay == 2:
            weight = jnp.concatenate([weight, swap(weight, "ay")], axis=0)
            order = lax.axis_index("ay")
            mine_all = jnp.concatenate(mine, axis=1)
            theirs_all = jnp.concatenate(theirs, axis=1)
            group = jnp.concatenate([mine_all, theirs_all], axis=0)
        else:
            group = lax.all_gather(jnp.concatenate(mine, axis=1), "ay", axis=0, tiled=True)
            weight = lax.all_gather(weight, "ay", axis=0, tiled=True)
        a = lax.axis_index("az") * n_ay + lax.axis_index("ay")
        own = lax.dynamic_slice_in_dim(group, a * width, width, axis=1)
        scaled = (weight[:, None] * own.astype(jnp.float32)).astype(jnp.bfloat16)
        partial_value = contract(scaled, group).reshape(width, n_rx, n_rc, rw)
        partial_value = reduce_pair(partial_value, "rc", n_rc, 2, jnp.float32)
        partial_value = reduce_pair(partial_value, "rx", n_rx, 1, jnp.bfloat16)
        return partial_value.reshape(width, rw)

    return body


def solution(mesh):
    n_rows = mesh.shape["rows"]
    n_aux = mesh.shape["aux"]
    n_rc = 2 if n_rows % 2 == 0 else 1
    n_ay = 2 if n_aux % 2 == 0 else 1
    n_rx = n_rows // n_rc
    n_az = n_aux // n_ay
    split = Mesh(mesh.devices.reshape(n_rx, n_rc, n_az, n_ay), ("rx", "rc", "az", "ay"))
    rows_all = ("rx", "rc", "az", "ay")
    placed = (P(rows_all, None), P(rows_all), P(), P(), P(), P())
    return jax.shard_map(
        make_body(n_rx, n_rc, n_az, n_ay),
        mesh=split,
        in_specs=placed,
        out_specs=P(("az", "ay"), ("rx", "rc")),
        check_vma=False,
    )
```

```python
import jax
import jax.numpy as jnp
from jax import lax
from jax.sharding import Mesh, PartitionSpec as P

NVIR = 1536
NOCC_B = 4


def row_weights(pairs, e_occ, e_vir, occ_batch, freq):
    batch_start = occ_batch[0] * NOCC_B
    e_batch = lax.dynamic_slice_in_dim(e_occ, batch_start, NOCC_B, 0)
    occ = pairs // NVIR
    vir = pairs % NVIR
    occ_hit = occ[:, None] == jnp.arange(NOCC_B, dtype=jnp.int32)[None, :]
    vir_hit = vir[:, None] == jnp.arange(e_vir.shape[0], dtype=jnp.int32)[None, :]
    e_low = jnp.sum(jnp.where(occ_hit, e_batch[None, :], 0.0), axis=1)
    e_high = jnp.sum(jnp.where(vir_hit, e_vir[None, :], 0.0), axis=1)
    delta = e_high - e_low
    return 2.0 * delta / (delta * delta + freq[0] * freq[0])


def contract(left, right):
    return lax.dot_general(
        left, right, (((0,), (0,)), ((), ())), preferred_element_type=jnp.float32
    )


def swap(x, axis):
    return lax.ppermute(x, axis, [(0, 1), (1, 0)])


def scale(weight, cols):
    return (weight[:, None] * cols.astype(jnp.float32)).astype(jnp.bfloat16)


def make_body(n_rx, n_rc, n_az, n_ay):
    def body(b_rows, pair_index, e_occ, e_vir, occ_batch, freq):
        nloc, naux = b_rows.shape
        width = naux // (n_az * n_ay)
        rw = naux // (n_rx * n_rc)
        z = lax.axis_index("az")
        x = lax.axis_index("rx")
        c = lax.axis_index("rc")
        a = z * n_ay + lax.axis_index("ay")
        order = [(1 - x) * 2 + (1 - c), x * 2 + (1 - c), (1 - x) * 2 + c, x * 2 + c]
        home = (a * width) // rw
        off = (a * width) % rw

        def others(v):
            doubled = jnp.concatenate([v, v], axis=0)
            return lax.dynamic_slice_in_dim(doubled, (z + 1) * nloc, (n_az - 1) * nloc, axis=0)

        def pick(blocks):
            out = lax.dynamic_slice_in_dim(blocks[0], off, width, axis=1)
            for k in range(1, len(blocks)):
                out = jnp.where(order[k] == home, lax.dynamic_slice_in_dim(blocks[k], off, width, axis=1), out)
            return out

        w_own = row_weights(pair_index, e_occ, e_vir, occ_batch, freq)
        w_a = swap(w_own, "ay")
        theirs_own = swap(b_rows, "ay")
        w_z = lax.all_gather(w_own, "az", axis=0, tiled=True)
        w_b = swap(others(w_z), "ay")
        mine, theirs = [], []
        for m in order:
            piece = lax.all_gather(
                lax.dynamic_slice_in_dim(b_rows, m * rw, rw, axis=1), "az", axis=0, tiled=True
            )
            mine.append(piece)
            theirs.append(swap(others(piece), "ay"))
        s_mine = scale(w_z, pick(mine))
        s_b = scale(w_b, pick(theirs))
        s_a = scale(w_a, lax.dynamic_slice_in_dim(theirs_own, a * width, width, axis=1))
        blocks = []
        for k, m in enumerate(order):
            cols_a = lax.dynamic_slice_in_dim(theirs_own, m * rw, rw, axis=1)
            blocks.append(contract(s_mine, mine[k]) + contract(s_b, theirs[k]) + contract(s_a, cols_a))
        got_other = swap(blocks[0], "rc")
        got_own = swap(blocks[1], "rc")
        other_x = blocks[2] + got_other
        got_x = swap(other_x.astype(jnp.bfloat16), "rx")
        return blocks[3] + got_own + got_x.astype(jnp.float32)

    return body


def make_plain_body(n_rows, n_aux):
    def body(b_rows, pair_index, e_occ, e_vir, occ_batch, freq):
        width = b_rows.shape[1] // n_aux
        group_pairs = lax.all_gather(pair_index, "aux", axis=0, tiled=True)
        group = lax.all_gather(b_rows, "aux", axis=0, tiled=True)
        own = lax.dynamic_slice_in_dim(group, lax.axis_index("aux") * width, width, axis=1)
        scaled = scale(row_weights(group_pairs, e_occ, e_vir, occ_batch, freq), own)
        return lax.psum_scatter(contract(scaled, group), "rows", scatter_dimension=1, tiled=True)

    return body


def solution(mesh):
    n_rows = mesh.shape["rows"]
    n_aux = mesh.shape["aux"]
    naux = 8192
    fits = n_rows == 4 and n_aux % 2 == 0 and (naux // n_rows) % (naux // n_aux) == 0
    if not fits:
        placed = (P(("rows", "aux"), None), P(("rows", "aux")), P(), P(), P(), P())
        return jax.shard_map(
            make_plain_body(n_rows, n_aux), mesh=mesh, in_specs=placed,
            out_specs=P("aux", "rows"), check_vma=False,
        )
    n_rx, n_rc, n_ay = 2, 2, 2
    n_az = n_aux // n_ay
    split = Mesh(mesh.devices.reshape(n_rx, n_rc, n_az, n_ay), ("rx", "rc", "az", "ay"))
    rows_all = ("rx", "rc", "az", "ay")
    placed = (P(rows_all, None), P(rows_all), P(), P(), P(), P())
    return jax.shard_map(
        make_body(n_rx, n_rc, n_az, n_ay),
        mesh=split,
        in_specs=placed,
        out_specs=P(("az", "ay"), ("rx", "rc")),
        check_vma=False,
    )
```

```python
import jax
import jax.numpy as jnp
from jax import lax
from jax.sharding import Mesh, PartitionSpec as P

NVIR = 1536
NOCC_B = 4


def row_weights(pairs, e_occ, e_vir, occ_batch, freq):
    batch_start = occ_batch[0] * NOCC_B
    e_batch = lax.dynamic_slice_in_dim(e_occ, batch_start, NOCC_B, 0)
    occ = pairs // NVIR
    vir = pairs % NVIR
    occ_hit = occ[:, None] == jnp.arange(NOCC_B, dtype=jnp.int32)[None, :]
    vir_hit = vir[:, None] == jnp.arange(e_vir.shape[0], dtype=jnp.int32)[None, :]
    e_low = jnp.sum(jnp.where(occ_hit, e_batch[None, :], 0.0), axis=1)
    e_high = jnp.sum(jnp.where(vir_hit, e_vir[None, :], 0.0), axis=1)
    delta = e_high - e_low
    return 2.0 * delta / (delta * delta + freq[0] * freq[0])


def contract(left, right):
    return lax.dot_general(
        left, right, (((0,), (0,)), ((), ())), preferred_element_type=jnp.float32
    )


def swap(x, axis):
    return lax.ppermute(x, axis, [(0, 1), (1, 0)])


def scale(weight, cols):
    return (weight[:, None] * cols.astype(jnp.float32)).astype(jnp.bfloat16)


def make_body(n_rx, n_rc, n_az, n_ay):
    def body(b_rows, pair_index, e_occ, e_vir, occ_batch, freq):
        nloc, naux = b_rows.shape
        width = naux // (n_az * n_ay)
        rw = naux // (n_rx * n_rc)
        z = lax.axis_index("az")
        x = lax.axis_index("rx")
        c = lax.axis_index("rc")
        a = z * n_ay + lax.axis_index("ay")
        order = [(1 - x) * 2 + (1 - c), x * 2 + (1 - c), (1 - x) * 2 + c, x * 2 + c]
        home = (a * width) // rw
        off = (a * width) % rw

        def others(v):
            doubled = jnp.concatenate([v, v], axis=0)
            return lax.dynamic_slice_in_dim(doubled, (z + 1) * nloc, (n_az - 1) * nloc, axis=0)

        def pick(blocks):
            out = lax.dynamic_slice_in_dim(blocks[0], off, width, axis=1)
            for k in range(1, len(blocks)):
                out = jnp.where(order[k] == home, lax.dynamic_slice_in_dim(blocks[k], off, width, axis=1), out)
            return out

        w_own = row_weights(pair_index, e_occ, e_vir, occ_batch, freq)
        w_z = lax.all_gather(w_own, "az", axis=0, tiled=True)
        first = lax.dynamic_slice_in_dim(b_rows, order[0] * rw, rw, axis=1)
        mine = [lax.all_gather(first, "az", axis=0, tiled=True)]
        w_a = swap(w_own, "ay")
        w_b = swap(others(w_z), "ay")
        theirs_own = swap(b_rows, "ay")
        theirs_own, w_a, w_b, rest = lax.optimization_barrier((theirs_own, w_a, w_b, b_rows))
        theirs = [swap(others(mine[0]), "ay")]
        for m in order[1:]:
            piece = lax.all_gather(
                lax.dynamic_slice_in_dim(rest, m * rw, rw, axis=1), "az", axis=0, tiled=True
            )
            mine.append(piece)
            theirs.append(swap(others(piece), "ay"))
        s_mine = scale(w_z, pick(mine))
        s_a = scale(w_a, lax.dynamic_slice_in_dim(theirs_own, a * width, width, axis=1))
        early = []
        for k, m in enumerate(order):
            cols_a = lax.dynamic_slice_in_dim(theirs_own, m * rw, rw, axis=1)
            early.append(contract(s_a, cols_a) + contract(s_mine, mine[k]))
        s_b = scale(w_b, pick(theirs))
        blocks = [early[k] + contract(s_b, theirs[k]) for k in range(len(order))]
        got_other = swap(blocks[0], "rc")
        other_x = blocks[2] + got_other
        got_x = swap(other_x.astype(jnp.bfloat16), "rx")
        got_own = swap(blocks[1], "rc")
        own_x = lax.optimization_barrier(blocks[3] + got_own)
        return own_x + got_x.astype(jnp.float32)

    return body


def make_plain_body(n_rows, n_aux):
    def body(b_rows, pair_index, e_occ, e_vir, occ_batch, freq):
        width = b_rows.shape[1] // n_aux
        group_pairs = lax.all_gather(pair_index, "aux", axis=0, tiled=True)
        group = lax.all_gather(b_rows, "aux", axis=0, tiled=True)
        own = lax.dynamic_slice_in_dim(group, lax.axis_index("aux") * width, width, axis=1)
        scaled = scale(row_weights(group_pairs, e_occ, e_vir, occ_batch, freq), own)
        return lax.psum_scatter(contract(scaled, group), "rows", scatter_dimension=1, tiled=True)

    return body


def solution(mesh):
    n_rows = mesh.shape["rows"]
    n_aux = mesh.shape["aux"]
    naux = 8192
    fits = n_rows == 4 and n_aux % 2 == 0 and (naux // n_rows) % (naux // n_aux) == 0
    if not fits:
        placed = (P(("rows", "aux"), None), P(("rows", "aux")), P(), P(), P(), P())
        return jax.shard_map(
            make_plain_body(n_rows, n_aux), mesh=mesh, in_specs=placed,
            out_specs=P("aux", "rows"), check_vma=False,
        )
    n_rx, n_rc, n_ay = 2, 2, 2
    n_az = n_aux // n_ay
    split = Mesh(mesh.devices.reshape(n_rx, n_rc, n_az, n_ay), ("rx", "rc", "az", "ay"))
    rows_all = ("rx", "rc", "az", "ay")
    placed = (P(rows_all, None), P(rows_all), P(), P(), P(), P())
    return jax.shard_map(
        make_body(n_rx, n_rc, n_az, n_ay),
        mesh=split,
        in_specs=placed,
        out_specs=P(("az", "ay"), ("rx", "rc")),
        check_vma=False,
    )
```

```python
import jax
import jax.numpy as jnp
from jax import lax
from jax.sharding import Mesh, PartitionSpec as P

NVIR = 1536
NOCC_B = 4


def row_weights(pairs, e_occ, e_vir, occ_batch, freq):
    batch_start = occ_batch[0] * NOCC_B
    e_batch = lax.dynamic_slice_in_dim(e_occ, batch_start, NOCC_B, 0)
    occ = pairs // NVIR
    vir = pairs % NVIR
    occ_hit = occ[:, None] == jnp.arange(NOCC_B, dtype=jnp.int32)[None, :]
    vir_hit = vir[:, None] == jnp.arange(e_vir.shape[0], dtype=jnp.int32)[None, :]
    e_low = jnp.sum(jnp.where(occ_hit, e_batch[None, :], 0.0), axis=1)
    e_high = jnp.sum(jnp.where(vir_hit, e_vir[None, :], 0.0), axis=1)
    delta = e_high - e_low
    return 2.0 * delta / (delta * delta + freq[0] * freq[0])


def contract(left, right):
    return lax.dot_general(
        left, right, (((0,), (0,)), ((), ())), preferred_element_type=jnp.float32
    )


def swap(x, axis):
    return lax.ppermute(x, axis, [(0, 1), (1, 0)])


def scale(weight, cols):
    return (weight[:, None] * cols.astype(jnp.float32)).astype(jnp.bfloat16)


def make_body(n_rx, n_rc, n_az, n_ay):
    def body(b_rows, pair_index, e_occ, e_vir, occ_batch, freq):
        nloc, naux = b_rows.shape
        width = naux // (n_az * n_ay)
        rw = naux // (n_rx * n_rc)
        z = lax.axis_index("az")
        x = lax.axis_index("rx")
        c = lax.axis_index("rc")
        a = z * n_ay + lax.axis_index("ay")
        order = [(1 - x) * 2 + (1 - c), (1 - x) * 2 + c, x * 2 + (1 - c), x * 2 + c]
        home = (a * width) // rw
        off = (a * width) % rw

        def others(v):
            doubled = jnp.concatenate([v, v], axis=0)
            return lax.dynamic_slice_in_dim(doubled, (z + 1) * nloc, (n_az - 1) * nloc, axis=0)

        def pick(blocks):
            out = lax.dynamic_slice_in_dim(blocks[0], off, width, axis=1)
            for k in range(1, len(blocks)):
                out = jnp.where(order[k] == home, lax.dynamic_slice_in_dim(blocks[k], off, width, axis=1), out)
            return out

        w_own = row_weights(pair_index, e_occ, e_vir, occ_batch, freq)
        w_z = lax.all_gather(w_own, "az", axis=0, tiled=True)
        first = lax.dynamic_slice_in_dim(b_rows, order[0] * rw, rw, axis=1)
        mine = [lax.all_gather(first, "az", axis=0, tiled=True)]
        w_a = swap(w_own, "ay")
        w_b = swap(others(w_z), "ay")
        theirs_own = swap(b_rows, "ay")
        theirs_own, w_a, w_b, rest = lax.optimization_barrier((theirs_own, w_a, w_b, b_rows))
        theirs = [swap(others(mine[0]), "ay")]
        for m in order[1:]:
            piece = lax.all_gather(
                lax.dynamic_slice_in_dim(rest, m * rw, rw, axis=1), "az", axis=0, tiled=True
            )
            mine.append(piece)
            theirs.append(swap(others(piece), "ay"))
        own_cols = [lax.dynamic_slice_in_dim(theirs_own, m * rw, rw, axis=1) for m in order]
        fwd = {}
        for k in (0, 2):
            fwd[k + 1] = [swap(own_cols[k], "rc"), swap(mine[k], "rc"), swap(theirs[k], "rc")]
        s_a = scale(w_a, lax.dynamic_slice_in_dim(theirs_own, a * width, width, axis=1))
        s_mine = scale(w_z, pick(mine))
        s_b = scale(w_b, pick(theirs))
        p_a = swap(s_a, "rc")
        p_mine = swap(s_mine, "rc")
        p_b = swap(s_b, "rc")
        kept = []
        for k in (1, 3):
            f_a, f_mine, f_b = fwd[k]
            early = (
                contract(s_a, own_cols[k]) + contract(s_mine, mine[k])
                + contract(p_a, f_a) + contract(p_mine, f_mine)
            )
            kept.append(early + contract(s_b, theirs[k]) + contract(p_b, f_b))
        got_x = swap(kept[0].astype(jnp.bfloat16), "rx")
        return kept[1] + got_x.astype(jnp.float32)

    return body


def make_plain_body(n_rows, n_aux):
    def body(b_rows, pair_index, e_occ, e_vir, occ_batch, freq):
        width = b_rows.shape[1] // n_aux
        group_pairs = lax.all_gather(pair_index, "aux", axis=0, tiled=True)
        group = lax.all_gather(b_rows, "aux", axis=0, tiled=True)
        own = lax.dynamic_slice_in_dim(group, lax.axis_index("aux") * width, width, axis=1)
        scaled = scale(row_weights(group_pairs, e_occ, e_vir, occ_batch, freq), own)
        return lax.psum_scatter(contract(scaled, group), "rows", scatter_dimension=1, tiled=True)

    return body


def solution(mesh):
    n_rows = mesh.shape["rows"]
    n_aux = mesh.shape["aux"]
    naux = 8192
    fits = n_rows == 4 and n_aux % 2 == 0 and (naux // n_rows) % (naux // n_aux) == 0
    if not fits:
        placed = (P(("rows", "aux"), None), P(("rows", "aux")), P(), P(), P(), P())
        return jax.shard_map(
            make_plain_body(n_rows, n_aux), mesh=mesh, in_specs=placed,
            out_specs=P("aux", "rows"), check_vma=False,
        )
    n_rx, n_rc, n_ay = 2, 2, 2
    n_az = n_aux // n_ay
    split = Mesh(mesh.devices.reshape(n_rx, n_rc, n_az, n_ay), ("rx", "rc", "az", "ay"))
    rows_all = ("rx", "rc", "az", "ay")
    placed = (P(rows_all, None), P(rows_all), P(), P(), P(), P())
    return jax.shard_map(
        make_body(n_rx, n_rc, n_az, n_ay),
        mesh=split,
        in_specs=placed,
        out_specs=P(("az", "ay"), ("rx", "rc")),
        check_vma=False,
    )
```

```python
import jax
import jax.numpy as jnp
from jax import lax
from jax.sharding import Mesh, PartitionSpec as P

NVIR = 1536
NOCC_B = 4


def row_weights(pairs, e_occ, e_vir, occ_batch, freq):
    batch_start = occ_batch[0] * NOCC_B
    e_batch = lax.dynamic_slice_in_dim(e_occ, batch_start, NOCC_B, 0)
    occ = pairs // NVIR
    vir = pairs % NVIR
    occ_hit = occ[:, None] == jnp.arange(NOCC_B, dtype=jnp.int32)[None, :]
    vir_hit = vir[:, None] == jnp.arange(e_vir.shape[0], dtype=jnp.int32)[None, :]
    e_low = jnp.sum(jnp.where(occ_hit, e_batch[None, :], 0.0), axis=1)
    e_high = jnp.sum(jnp.where(vir_hit, e_vir[None, :], 0.0), axis=1)
    delta = e_high - e_low
    return 2.0 * delta / (delta * delta + freq[0] * freq[0])


def contract(left, right):
    return lax.dot_general(
        left, right, (((0,), (0,)), ((), ())), preferred_element_type=jnp.float32
    )


def swap(x, axis):
    return lax.ppermute(x, axis, [(0, 1), (1, 0)])


def scale(weight, cols):
    return (weight[:, None] * cols.astype(jnp.float32)).astype(jnp.bfloat16)


def make_body(n_rx, n_rc, n_az, n_ay):
    def body(b_rows, pair_index, e_occ, e_vir, occ_batch, freq):
        nloc, naux = b_rows.shape
        width = naux // (n_az * n_ay)
        rw = naux // (n_rx * n_rc)
        z = lax.axis_index("az")
        x = lax.axis_index("rx")
        c = lax.axis_index("rc")
        a = z * n_ay + lax.axis_index("ay")
        order = [(1 - x) * 2 + (1 - c), x * 2 + (1 - c), (1 - x) * 2 + c, x * 2 + c]
        home = (a * width) // rw
        off = (a * width) % rw

        def others(v):
            doubled = jnp.concatenate([v, v], axis=0)
            return lax.dynamic_slice_in_dim(doubled, (z + 1) * nloc, (n_az - 1) * nloc, axis=0)

        def pick(blocks):
            out = lax.dynamic_slice_in_dim(blocks[0], off, width, axis=1)
            for k in range(1, len(blocks)):
                out = jnp.where(order[k] == home, lax.dynamic_slice_in_dim(blocks[k], off, width, axis=1), out)
            return out

        w_own = row_weights(pair_index, e_occ, e_vir, occ_batch, freq)
        w_z = lax.all_gather(w_own, "az", axis=0, tiled=True)
        first = lax.dynamic_slice_in_dim(b_rows, order[0] * rw, rw, axis=1)
        mine = [lax.all_gather(first, "az", axis=0, tiled=True)]
        w_a = swap(w_own, "ay")
        w_b = swap(others(w_z), "ay")
        theirs_own = swap(b_rows, "ay")
        theirs_own, w_a, w_b, rest = lax.optimization_barrier((theirs_own, w_a, w_b, b_rows))
        theirs = [swap(others(mine[0]), "ay")]
        for m in order[1:]:
            piece = lax.all_gather(
                lax.dynamic_slice_in_dim(rest, m * rw, rw, axis=1), "az", axis=0, tiled=True
            )
            mine.append(piece)
            theirs.append(swap(others(piece), "ay"))
        s_mine = scale(w_z, pick(mine))
        s_a = scale(w_a, lax.dynamic_slice_in_dim(theirs_own, a * width, width, axis=1))
        early = []
        for k, m in enumerate(order):
            cols_a = lax.dynamic_slice_in_dim(theirs_own, m * rw, rw, axis=1)
            early.append(contract(s_a, cols_a) + contract(s_mine, mine[k]))
        s_b = scale(w_b, pick(theirs))
        halves = 2 if width % 16 == 0 else 1
        hw = width // halves
        outs = []
        for h in range(halves):
            rows = slice(h * hw, (h + 1) * hw)
            s_h = s_b[:, rows]
            blocks = [early[k][rows] + contract(s_h, theirs[k]) for k in range(len(order))]
            got_other = swap(blocks[0], "rc")
            other_x = blocks[2] + got_other
            got_x = swap(other_x.astype(jnp.bfloat16), "rx")
            got_own = swap(blocks[1], "rc")
            own_x = lax.optimization_barrier(blocks[3] + got_own)
            outs.append(own_x + got_x.astype(jnp.float32))
        return jnp.concatenate(outs, axis=0) if halves > 1 else outs[0]

    return body


def make_plain_body(n_rows, n_aux):
    def body(b_rows, pair_index, e_occ, e_vir, occ_batch, freq):
        width = b_rows.shape[1] // n_aux
        group_pairs = lax.all_gather(pair_index, "aux", axis=0, tiled=True)
        group = lax.all_gather(b_rows, "aux", axis=0, tiled=True)
        own = lax.dynamic_slice_in_dim(group, lax.axis_index("aux") * width, width, axis=1)
        scaled = scale(row_weights(group_pairs, e_occ, e_vir, occ_batch, freq), own)
        return lax.psum_scatter(contract(scaled, group), "rows", scatter_dimension=1, tiled=True)

    return body


def solution(mesh):
    n_rows = mesh.shape["rows"]
    n_aux = mesh.shape["aux"]
    naux = 8192
    fits = n_rows == 4 and n_aux % 2 == 0 and (naux // n_rows) % (naux // n_aux) == 0
    if not fits:
        placed = (P(("rows", "aux"), None), P(("rows", "aux")), P(), P(), P(), P())
        return jax.shard_map(
            make_plain_body(n_rows, n_aux), mesh=mesh, in_specs=placed,
            out_specs=P("aux", "rows"), check_vma=False,
        )
    n_rx, n_rc, n_ay = 2, 2, 2
    n_az = n_aux // n_ay
    split = Mesh(mesh.devices.reshape(n_rx, n_rc, n_az, n_ay), ("rx", "rc", "az", "ay"))
    rows_all = ("rx", "rc", "az", "ay")
    placed = (P(rows_all, None), P(rows_all), P(), P(), P(), P())
    return jax.shard_map(
        make_body(n_rx, n_rc, n_az, n_ay),
        mesh=split,
        in_specs=placed,
        out_specs=P(("az", "ay"), ("rx", "rc")),
        check_vma=False,
    )
```

```python
import jax
import jax.numpy as jnp
from jax import lax
from jax.sharding import Mesh, PartitionSpec as P

NVIR = 1536
NOCC_B = 4


def row_weights(pairs, e_occ, e_vir, occ_batch, freq):
    batch_start = occ_batch[0] * NOCC_B
    e_batch = lax.dynamic_slice_in_dim(e_occ, batch_start, NOCC_B, 0)
    occ = pairs // NVIR
    vir = pairs % NVIR
    occ_hit = occ[:, None] == jnp.arange(NOCC_B, dtype=jnp.int32)[None, :]
    vir_hit = vir[:, None] == jnp.arange(e_vir.shape[0], dtype=jnp.int32)[None, :]
    e_low = jnp.sum(jnp.where(occ_hit, e_batch[None, :], 0.0), axis=1)
    e_high = jnp.sum(jnp.where(vir_hit, e_vir[None, :], 0.0), axis=1)
    delta = e_high - e_low
    return 2.0 * delta / (delta * delta + freq[0] * freq[0])


def contract(left, right):
    return lax.dot_general(
        left, right, (((0,), (0,)), ((), ())), preferred_element_type=jnp.float32
    )


def swap(x, axis):
    return lax.ppermute(x, axis, [(0, 1), (1, 0)])


def scale(weight, cols):
    return (weight[:, None] * cols.astype(jnp.float32)).astype(jnp.bfloat16)


def make_body(n_rx, n_rc, n_az, n_ay):
    def body(b_rows, pair_index, e_occ, e_vir, occ_batch, freq):
        nloc, naux = b_rows.shape
        width = naux // (n_az * n_ay)
        rw = naux // (n_rx * n_rc)
        z = lax.axis_index("az")
        x = lax.axis_index("rx")
        c = lax.axis_index("rc")
        a = z * n_ay + lax.axis_index("ay")
        order = [(1 - x) * 2 + (1 - c), x * 2 + (1 - c), (1 - x) * 2 + c, x * 2 + c]
        home = (a * width) // rw
        off = (a * width) % rw

        def others(v):
            doubled = jnp.concatenate([v, v], axis=0)
            return lax.dynamic_slice_in_dim(doubled, (z + 1) * nloc, (n_az - 1) * nloc, axis=0)

        def pick(blocks):
            out = lax.dynamic_slice_in_dim(blocks[0], off, width, axis=1)
            for k in range(1, len(blocks)):
                out = jnp.where(order[k] == home, lax.dynamic_slice_in_dim(blocks[k], off, width, axis=1), out)
            return out

        w_own = row_weights(pair_index, e_occ, e_vir, occ_batch, freq)
        w_z = lax.all_gather(w_own, "az", axis=0, tiled=True)
        first = lax.dynamic_slice_in_dim(b_rows, order[0] * rw, rw, axis=1)
        mine = [lax.all_gather(first, "az", axis=0, tiled=True)]
        w_a = swap(w_own, "ay")
        w_b = swap(others(w_z), "ay")
        theirs_own = swap(b_rows, "ay")
        theirs_own, w_a, w_b, rest = lax.optimization_barrier((theirs_own, w_a, w_b, b_rows))
        theirs = [swap(others(mine[0]), "ay")]
        for k, m in enumerate(order[1:], start=1):
            parts = 2 if (k == len(order) - 1 and rw % 256 == 0) else 1
            pw = rw // parts
            got_mine, got_theirs = [], []
            for p in range(parts):
                piece = lax.all_gather(
                    lax.dynamic_slice_in_dim(rest, m * rw + p * pw, pw, axis=1), "az", axis=0, tiled=True
                )
                got_mine.append(piece)
                got_theirs.append(swap(others(piece), "ay"))
            mine.append(jnp.concatenate(got_mine, axis=1) if parts > 1 else got_mine[0])
            theirs.append(jnp.concatenate(got_theirs, axis=1) if parts > 1 else got_theirs[0])
        s_mine = scale(w_z, pick(mine))
        s_a = scale(w_a, lax.dynamic_slice_in_dim(theirs_own, a * width, width, axis=1))
        early = []
        for k, m in enumerate(order):
            cols_a = lax.dynamic_slice_in_dim(theirs_own, m * rw, rw, axis=1)
            early.append(contract(s_a, cols_a) + contract(s_mine, mine[k]))
        s_b = scale(w_b, pick(theirs))
        halves = 2 if width % 16 == 0 else 1
        hw = width // halves
        outs = []
        for h in range(halves):
            rows = slice(h * hw, (h + 1) * hw)
            s_h = s_b[:, rows]
            blocks = [early[k][rows] + contract(s_h, theirs[k]) for k in range(len(order))]
            got_other = swap(blocks[0], "rc")
            other_x = blocks[2] + got_other
            got_x = swap(other_x.astype(jnp.bfloat16), "rx")
            got_own = swap(blocks[1], "rc")
            own_x = lax.optimization_barrier(blocks[3] + got_own)
            outs.append(own_x + got_x.astype(jnp.float32))
        return jnp.concatenate(outs, axis=0) if halves > 1 else outs[0]

    return body


def make_plain_body(n_rows, n_aux):
    def body(b_rows, pair_index, e_occ, e_vir, occ_batch, freq):
        width = b_rows.shape[1] // n_aux
        group_pairs = lax.all_gather(pair_index, "aux", axis=0, tiled=True)
        group = lax.all_gather(b_rows, "aux", axis=0, tiled=True)
        own = lax.dynamic_slice_in_dim(group, lax.axis_index("aux") * width, width, axis=1)
        scaled = scale(row_weights(group_pairs, e_occ, e_vir, occ_batch, freq), own)
        return lax.psum_scatter(contract(scaled, group), "rows", scatter_dimension=1, tiled=True)

    return body


def solution(mesh):
    n_rows = mesh.shape["rows"]
    n_aux = mesh.shape["aux"]
    naux = 8192
    fits = n_rows == 4 and n_aux % 2 == 0 and (naux // n_rows) % (naux // n_aux) == 0
    if not fits:
        placed = (P(("rows", "aux"), None), P(("rows", "aux")), P(), P(), P(), P())
        return jax.shard_map(
            make_plain_body(n_rows, n_aux), mesh=mesh, in_specs=placed,
            out_specs=P("aux", "rows"), check_vma=False,
        )
    n_rx, n_rc, n_ay = 2, 2, 2
    n_az = n_aux // n_ay
    split = Mesh(mesh.devices.reshape(n_rx, n_rc, n_az, n_ay), ("rx", "rc", "az", "ay"))
    rows_all = ("rx", "rc", "az", "ay")
    placed = (P(rows_all, None), P(rows_all), P(), P(), P(), P())
    return jax.shard_map(
        make_body(n_rx, n_rc, n_az, n_ay),
        mesh=split,
        in_specs=placed,
        out_specs=P(("az", "ay"), ("rx", "rc")),
        check_vma=False,
    )
```

```python
import jax
import jax.numpy as jnp
from jax import lax
from jax.sharding import Mesh, PartitionSpec as P

NVIR = 1536
NOCC_B = 4


def row_weights(pairs, e_occ, e_vir, occ_batch, freq):
    batch_start = occ_batch[0] * NOCC_B
    e_batch = lax.dynamic_slice_in_dim(e_occ, batch_start, NOCC_B, 0)
    occ = pairs // NVIR
    vir = pairs % NVIR
    occ_hit = occ[:, None] == jnp.arange(NOCC_B, dtype=jnp.int32)[None, :]
    vir_hit = vir[:, None] == jnp.arange(e_vir.shape[0], dtype=jnp.int32)[None, :]
    e_low = jnp.sum(jnp.where(occ_hit, e_batch[None, :], 0.0), axis=1)
    e_high = jnp.sum(jnp.where(vir_hit, e_vir[None, :], 0.0), axis=1)
    delta = e_high - e_low
    return 2.0 * delta / (delta * delta + freq[0] * freq[0])


def contract(left, right):
    return lax.dot_general(
        left, right, (((0,), (0,)), ((), ())), preferred_element_type=jnp.float32
    )


def swap(x, axis):
    return lax.ppermute(x, axis, [(0, 1), (1, 0)])


def scale(weight, cols):
    return (weight[:, None] * cols.astype(jnp.float32)).astype(jnp.bfloat16)


def make_body(n_rx, n_rc, n_az, n_ay):
    def body(b_rows, pair_index, e_occ, e_vir, occ_batch, freq):
        nloc, naux = b_rows.shape
        width = naux // (n_az * n_ay)
        rw = naux // (n_rx * n_rc)
        z = lax.axis_index("az")
        x = lax.axis_index("rx")
        c = lax.axis_index("rc")
        a = z * n_ay + lax.axis_index("ay")
        order = [(1 - x) * 2 + (1 - c), x * 2 + (1 - c), (1 - x) * 2 + c, x * 2 + c]
        home = (a * width) // rw
        off = (a * width) % rw

        def others(v):
            doubled = jnp.concatenate([v, v], axis=0)
            return lax.dynamic_slice_in_dim(doubled, (z + 1) * nloc, (n_az - 1) * nloc, axis=0)

        def pick(blocks):
            out = lax.dynamic_slice_in_dim(blocks[0], off, width, axis=1)
            for k in range(1, len(blocks)):
                out = jnp.where(order[k] == home, lax.dynamic_slice_in_dim(blocks[k], off, width, axis=1), out)
            return out

        w_own = row_weights(pair_index, e_occ, e_vir, occ_batch, freq)
        w_z = lax.all_gather(w_own, "az", axis=0, tiled=True)
        first = lax.dynamic_slice_in_dim(b_rows, order[0] * rw, rw, axis=1)
        mine = [lax.all_gather(first, "az", axis=0, tiled=True)]
        w_a = swap(w_own, "ay")
        w_b = swap(others(w_z), "ay")
        theirs_own = swap(b_rows, "ay")
        theirs_own, w_a, w_b, rest = lax.optimization_barrier((theirs_own, w_a, w_b, b_rows))
        theirs = [swap(others(mine[0]), "ay")]
        pieces = []
        for k, m in enumerate(order[1:], start=1):
            parts = 2 if (k == len(order) - 1 and rw % 256 == 0) else 1
            pieces += [(k, m * rw + p * (rw // parts), rw // parts) for p in range(parts)]
        got_mine, got_theirs = [mine[0]], [theirs[0]]
        by_block = {}
        for k, start, pw in pieces:
            _, _, rest = lax.optimization_barrier((got_mine[-1], got_theirs[-2] if len(got_theirs) > 1 else w_a, rest))
            piece = lax.all_gather(lax.dynamic_slice_in_dim(rest, start, pw, axis=1), "az", axis=0, tiled=True)
            got_mine.append(piece)
            got_theirs.append(swap(others(piece), "ay"))
            by_block.setdefault(k, []).append(len(got_mine) - 1)
        for k in range(1, len(order)):
            idx = by_block[k]
            mine.append(jnp.concatenate([got_mine[i] for i in idx], axis=1) if len(idx) > 1 else got_mine[idx[0]])
            theirs.append(jnp.concatenate([got_theirs[i] for i in idx], axis=1) if len(idx) > 1 else got_theirs[idx[0]])
        s_mine = scale(w_z, pick(mine))
        s_a = scale(w_a, lax.dynamic_slice_in_dim(theirs_own, a * width, width, axis=1))
        early = []
        for k, m in enumerate(order):
            cols_a = lax.dynamic_slice_in_dim(theirs_own, m * rw, rw, axis=1)
            early.append(contract(s_a, cols_a) + contract(s_mine, mine[k]))
        s_b = scale(w_b, pick(theirs))
        halves = 2 if width % 16 == 0 else 1
        hw = width // halves
        outs = []
        for h in range(halves):
            rows = slice(h * hw, (h + 1) * hw)
            s_h = s_b[:, rows]
            blocks = [early[k][rows] + contract(s_h, theirs[k]) for k in range(len(order))]
            got_other = swap(blocks[0], "rc")
            other_x = blocks[2] + got_other
            got_x = swap(other_x.astype(jnp.bfloat16), "rx")
            got_own = swap(blocks[1], "rc")
            own_x = lax.optimization_barrier(blocks[3] + got_own)
            outs.append(own_x + got_x.astype(jnp.float32))
        return jnp.concatenate(outs, axis=0) if halves > 1 else outs[0]

    return body


def make_plain_body(n_rows, n_aux):
    def body(b_rows, pair_index, e_occ, e_vir, occ_batch, freq):
        width = b_rows.shape[1] // n_aux
        group_pairs = lax.all_gather(pair_index, "aux", axis=0, tiled=True)
        group = lax.all_gather(b_rows, "aux", axis=0, tiled=True)
        own = lax.dynamic_slice_in_dim(group, lax.axis_index("aux") * width, width, axis=1)
        scaled = scale(row_weights(group_pairs, e_occ, e_vir, occ_batch, freq), own)
        return lax.psum_scatter(contract(scaled, group), "rows", scatter_dimension=1, tiled=True)

    return body


def solution(mesh):
    n_rows = mesh.shape["rows"]
    n_aux = mesh.shape["aux"]
    naux = 8192
    fits = n_rows == 4 and n_aux % 2 == 0 and (naux // n_rows) % (naux // n_aux) == 0
    if not fits:
        placed = (P(("rows", "aux"), None), P(("rows", "aux")), P(), P(), P(), P())
        return jax.shard_map(
            make_plain_body(n_rows, n_aux), mesh=mesh, in_specs=placed,
            out_specs=P("aux", "rows"), check_vma=False,
        )
    n_rx, n_rc, n_ay = 2, 2, 2
    n_az = n_aux // n_ay
    split = Mesh(mesh.devices.reshape(n_rx, n_rc, n_az, n_ay), ("rx", "rc", "az", "ay"))
    rows_all = ("rx", "rc", "az", "ay")
    placed = (P(rows_all, None), P(rows_all), P(), P(), P(), P())
    return jax.shard_map(
        make_body(n_rx, n_rc, n_az, n_ay),
        mesh=split,
        in_specs=placed,
        out_specs=P(("az", "ay"), ("rx", "rc")),
        check_vma=False,
    )
```

```python
import jax
import jax.numpy as jnp
from jax import lax
from jax.sharding import Mesh, PartitionSpec as P

NVIR = 1536
NOCC_B = 4


def row_weights(pairs, e_occ, e_vir, occ_batch, freq):
    batch_start = occ_batch[0] * NOCC_B
    e_batch = lax.dynamic_slice_in_dim(e_occ, batch_start, NOCC_B, 0)
    occ = pairs // NVIR
    vir = pairs % NVIR
    occ_hit = occ[:, None] == jnp.arange(NOCC_B, dtype=jnp.int32)[None, :]
    vir_hit = vir[:, None] == jnp.arange(e_vir.shape[0], dtype=jnp.int32)[None, :]
    e_low = jnp.sum(jnp.where(occ_hit, e_batch[None, :], 0.0), axis=1)
    e_high = jnp.sum(jnp.where(vir_hit, e_vir[None, :], 0.0), axis=1)
    delta = e_high - e_low
    return 2.0 * delta / (delta * delta + freq[0] * freq[0])


def contract(left, right):
    return lax.dot_general(
        left, right, (((0,), (0,)), ((), ())), preferred_element_type=jnp.float32
    )


def swap(x, axis):
    return lax.ppermute(x, axis, [(0, 1), (1, 0)])


def scale(weight, cols):
    return (weight[:, None] * cols.astype(jnp.float32)).astype(jnp.bfloat16)


def make_body(n_rx, n_rc, n_az, n_ay):
    def body(b_rows, pair_index, e_occ, e_vir, occ_batch, freq):
        nloc, naux = b_rows.shape
        width = naux // (n_az * n_ay)
        rw = naux // (n_rx * n_rc)
        z = lax.axis_index("az")
        x = lax.axis_index("rx")
        c = lax.axis_index("rc")
        a = z * n_ay + lax.axis_index("ay")
        order = [(1 - x) * 2 + (1 - c), x * 2 + (1 - c), (1 - x) * 2 + c, x * 2 + c]
        home = (a * width) // rw
        off = (a * width) % rw

        def others(v):
            doubled = jnp.concatenate([v, v], axis=0)
            return lax.dynamic_slice_in_dim(doubled, (z + 1) * nloc, (n_az - 1) * nloc, axis=0)

        def pick(blocks):
            out = lax.dynamic_slice_in_dim(blocks[0], off, width, axis=1)
            for k in range(1, len(blocks)):
                out = jnp.where(order[k] == home, lax.dynamic_slice_in_dim(blocks[k], off, width, axis=1), out)
            return out

        w_own = row_weights(pair_index, e_occ, e_vir, occ_batch, freq)
        w_z = lax.all_gather(w_own, "az", axis=0, tiled=True)
        first = lax.dynamic_slice_in_dim(b_rows, order[0] * rw, rw, axis=1)
        mine = [lax.all_gather(first, "az", axis=0, tiled=True)]
        w_a = swap(w_own, "ay")
        w_b = swap(others(w_z), "ay")
        theirs_own = swap(b_rows, "ay")
        theirs_own, w_a, w_b, rest = lax.optimization_barrier((theirs_own, w_a, w_b, b_rows))
        theirs = [swap(others(mine[0]), "ay")]
        pieces = []
        for k, m in enumerate(order[1:], start=1):
            parts = 2 if (k == len(order) - 1 and rw % 256 == 0) else 1
            pieces += [(k, m * rw + p * (rw // parts), rw // parts) for p in range(parts)]
        got_mine, got_theirs = [mine[0]], [theirs[0]]
        by_block = {}
        for k, start, pw in pieces:
            _, _, rest = lax.optimization_barrier((got_mine[-1], got_theirs[-3] if len(got_theirs) > 2 else w_a, rest))
            piece = lax.all_gather(lax.dynamic_slice_in_dim(rest, start, pw, axis=1), "az", axis=0, tiled=True)
            got_mine.append(piece)
            got_theirs.append(swap(others(piece), "ay"))
            by_block.setdefault(k, []).append(len(got_mine) - 1)
        for k in range(1, len(order)):
            idx = by_block[k]
            mine.append(jnp.concatenate([got_mine[i] for i in idx], axis=1) if len(idx) > 1 else got_mine[idx[0]])
            theirs.append(jnp.concatenate([got_theirs[i] for i in idx], axis=1) if len(idx) > 1 else got_theirs[idx[0]])
        s_mine = scale(w_z, pick(mine))
        s_a = scale(w_a, lax.dynamic_slice_in_dim(theirs_own, a * width, width, axis=1))
        early = []
        for k, m in enumerate(order):
            cols_a = lax.dynamic_slice_in_dim(theirs_own, m * rw, rw, axis=1)
            early.append(contract(s_a, cols_a) + contract(s_mine, mine[k]))
        s_b = scale(w_b, pick(theirs))
        halves = 2 if width % 16 == 0 else 1
        hw = width // halves
        cuts = [slice(h * hw, (h + 1) * hw) for h in range(halves)]
        sent, got_x = [], []
        for rows in cuts:
            s_h = s_b[:, rows]
            give = early[0][rows] + contract(s_h, theirs[0])
            other_x = early[2][rows] + contract(s_h, theirs[2]) + swap(give, "rc")
            sent.append(other_x.astype(jnp.bfloat16))
            got_x.append(swap(sent[-1], "rx"))
        _, late_give, late_keep, t_give, t_keep = lax.optimization_barrier(
            (tuple(sent), early[1], early[3], theirs[1], theirs[3])
        )
        outs = []
        for h, rows in enumerate(cuts):
            s_h = s_b[:, rows]
            give = late_give[rows] + contract(s_h, t_give)
            own_x = late_keep[rows] + contract(s_h, t_keep) + swap(give, "rc")
            outs.append(own_x + got_x[h].astype(jnp.float32))
        return jnp.concatenate(outs, axis=0) if halves > 1 else outs[0]

    return body


def make_plain_body(n_rows, n_aux):
    def body(b_rows, pair_index, e_occ, e_vir, occ_batch, freq):
        width = b_rows.shape[1] // n_aux
        group_pairs = lax.all_gather(pair_index, "aux", axis=0, tiled=True)
        group = lax.all_gather(b_rows, "aux", axis=0, tiled=True)
        own = lax.dynamic_slice_in_dim(group, lax.axis_index("aux") * width, width, axis=1)
        scaled = scale(row_weights(group_pairs, e_occ, e_vir, occ_batch, freq), own)
        return lax.psum_scatter(contract(scaled, group), "rows", scatter_dimension=1, tiled=True)

    return body


def solution(mesh):
    n_rows = mesh.shape["rows"]
    n_aux = mesh.shape["aux"]
    naux = 8192
    fits = n_rows == 4 and n_aux % 2 == 0 and (naux // n_rows) % (naux // n_aux) == 0
    if not fits:
        placed = (P(("rows", "aux"), None), P(("rows", "aux")), P(), P(), P(), P())
        return jax.shard_map(
            make_plain_body(n_rows, n_aux), mesh=mesh, in_specs=placed,
            out_specs=P("aux", "rows"), check_vma=False,
        )
    n_rx, n_rc, n_ay = 2, 2, 2
    n_az = n_aux // n_ay
    split = Mesh(mesh.devices.reshape(n_rx, n_rc, n_az, n_ay), ("rx", "rc", "az", "ay"))
    rows_all = ("rx", "rc", "az", "ay")
    placed = (P(rows_all, None), P(rows_all), P(), P(), P(), P())
    return jax.shard_map(
        make_body(n_rx, n_rc, n_az, n_ay),
        mesh=split,
        in_specs=placed,
        out_specs=P(("az", "ay"), ("rx", "rc")),
        check_vma=False,
    )
```

```python
import jax
import jax.numpy as jnp
from jax import lax
from jax.sharding import Mesh, PartitionSpec as P

NVIR = 1536
NOCC_B = 4


def row_weights(pairs, e_occ, e_vir, occ_batch, freq):
    batch_start = occ_batch[0] * NOCC_B
    e_batch = lax.dynamic_slice_in_dim(e_occ, batch_start, NOCC_B, 0)
    occ = pairs // NVIR
    vir = pairs % NVIR
    occ_hit = occ[:, None] == jnp.arange(NOCC_B, dtype=jnp.int32)[None, :]
    vir_hit = vir[:, None] == jnp.arange(e_vir.shape[0], dtype=jnp.int32)[None, :]
    e_low = jnp.sum(jnp.where(occ_hit, e_batch[None, :], 0.0), axis=1)
    e_high = jnp.sum(jnp.where(vir_hit, e_vir[None, :], 0.0), axis=1)
    delta = e_high - e_low
    return 2.0 * delta / (delta * delta + freq[0] * freq[0])


def contract(left, right):
    return lax.dot_general(
        left, right, (((0,), (0,)), ((), ())), preferred_element_type=jnp.float32
    )


def swap(x, axis):
    return lax.ppermute(x, axis, [(0, 1), (1, 0)])


def scale(weight, cols):
    return (weight[:, None] * cols.astype(jnp.float32)).astype(jnp.bfloat16)


def make_body(n_rx, n_rc, n_az, n_ay):
    def body(b_rows, pair_index, e_occ, e_vir, occ_batch, freq):
        nloc, naux = b_rows.shape
        width = naux // (n_az * n_ay)
        rw = naux // (n_rx * n_rc)
        z = lax.axis_index("az")
        x = lax.axis_index("rx")
        c = lax.axis_index("rc")
        a = z * n_ay + lax.axis_index("ay")
        order = [(1 - x) * 2 + (1 - c), x * 2 + (1 - c), (1 - x) * 2 + c, x * 2 + c]
        home = (a * width) // rw
        off = (a * width) % rw

        def others(v):
            doubled = jnp.concatenate([v, v], axis=0)
            return lax.dynamic_slice_in_dim(doubled, (z + 1) * nloc, (n_az - 1) * nloc, axis=0)

        def pick(blocks):
            out = lax.dynamic_slice_in_dim(blocks[0], off, width, axis=1)
            for k in range(1, len(blocks)):
                out = jnp.where(order[k] == home, lax.dynamic_slice_in_dim(blocks[k], off, width, axis=1), out)
            return out

        w_own = row_weights(pair_index, e_occ, e_vir, occ_batch, freq)
        w_z = lax.all_gather(w_own, "az", axis=0, tiled=True)
        first = lax.dynamic_slice_in_dim(b_rows, order[0] * rw, rw, axis=1)
        mine = [lax.all_gather(first, "az", axis=0, tiled=True)]
        w_a = swap(w_own, "ay")
        w_b = swap(others(w_z), "ay")
        theirs_own = swap(b_rows, "ay")
        theirs_own, w_a, w_b, rest = lax.optimization_barrier((theirs_own, w_a, w_b, b_rows))
        theirs = [swap(others(mine[0]), "ay")]
        pieces = []
        for k, m in enumerate(order[1:], start=1):
            parts = 1
            pieces += [(k, m * rw + p * (rw // parts), rw // parts) for p in range(parts)]
        got_mine, got_theirs = [mine[0]], [theirs[0]]
        by_block = {}
        for k, start, pw in pieces:
            _, _, rest = lax.optimization_barrier((got_mine[-1], got_theirs[-2] if len(got_theirs) > 1 else w_a, rest))
            piece = lax.all_gather(lax.dynamic_slice_in_dim(rest, start, pw, axis=1), "az", axis=0, tiled=True)
            got_mine.append(piece)
            got_theirs.append(swap(others(piece), "ay"))
            by_block.setdefault(k, []).append(len(got_mine) - 1)
        for k in range(1, len(order)):
            idx = by_block[k]
            mine.append(jnp.concatenate([got_mine[i] for i in idx], axis=1) if len(idx) > 1 else got_mine[idx[0]])
            theirs.append(jnp.concatenate([got_theirs[i] for i in idx], axis=1) if len(idx) > 1 else got_theirs[idx[0]])
        s_mine = scale(w_z, pick(mine))
        s_a = scale(w_a, lax.dynamic_slice_in_dim(theirs_own, a * width, width, axis=1))
        early = []
        for k, m in enumerate(order):
            cols_a = lax.dynamic_slice_in_dim(theirs_own, m * rw, rw, axis=1)
            early.append(contract(s_a, cols_a) + contract(s_mine, mine[k]))
        s_b = scale(w_b, pick(theirs))
        halves = 2 if width % 16 == 0 else 1
        hw = width // halves
        cuts = [slice(h * hw, (h + 1) * hw) for h in range(halves)]
        sent, got_x = [], []
        for rows in cuts:
            s_h = s_b[:, rows]
            give = early[0][rows] + contract(s_h, theirs[0])
            other_x = early[2][rows] + contract(s_h, theirs[2]) + swap(give, "rc")
            sent.append(other_x.astype(jnp.bfloat16))
            got_x.append(swap(sent[-1], "rx"))
        _, late_give, late_keep, t_give, t_keep = lax.optimization_barrier(
            (tuple(sent), early[1], early[3], theirs[1], theirs[3])
        )
        outs = []
        for h, rows in enumerate(cuts):
            s_h = s_b[:, rows]
            give = late_give[rows] + contract(s_h, t_give)
            own_x = late_keep[rows] + contract(s_h, t_keep) + swap(give, "rc")
            outs.append(own_x + got_x[h].astype(jnp.float32))
        return jnp.concatenate(outs, axis=0) if halves > 1 else outs[0]

    return body


def make_plain_body(n_rows, n_aux):
    def body(b_rows, pair_index, e_occ, e_vir, occ_batch, freq):
        width = b_rows.shape[1] // n_aux
        group_pairs = lax.all_gather(pair_index, "aux", axis=0, tiled=True)
        group = lax.all_gather(b_rows, "aux", axis=0, tiled=True)
        own = lax.dynamic_slice_in_dim(group, lax.axis_index("aux") * width, width, axis=1)
        scaled = scale(row_weights(group_pairs, e_occ, e_vir, occ_batch, freq), own)
        return lax.psum_scatter(contract(scaled, group), "rows", scatter_dimension=1, tiled=True)

    return body


def solution(mesh):
    n_rows = mesh.shape["rows"]
    n_aux = mesh.shape["aux"]
    naux = 8192
    fits = n_rows == 4 and n_aux % 2 == 0 and (naux // n_rows) % (naux // n_aux) == 0
    if not fits:
        placed = (P(("rows", "aux"), None), P(("rows", "aux")), P(), P(), P(), P())
        return jax.shard_map(
            make_plain_body(n_rows, n_aux), mesh=mesh, in_specs=placed,
            out_specs=P("aux", "rows"), check_vma=False,
        )
    n_rx, n_rc, n_ay = 2, 2, 2
    n_az = n_aux // n_ay
    split = Mesh(mesh.devices.reshape(n_rx, n_rc, n_az, n_ay), ("rx", "rc", "az", "ay"))
    rows_all = ("rx", "rc", "az", "ay")
    placed = (P(rows_all, None), P(rows_all), P(), P(), P(), P())
    return jax.shard_map(
        make_body(n_rx, n_rc, n_az, n_ay),
        mesh=split,
        in_specs=placed,
        out_specs=P(("az", "ay"), ("rx", "rc")),
        check_vma=False,
    )
```

```python
import jax
import jax.numpy as jnp
from jax import lax
from jax.sharding import Mesh, PartitionSpec as P

NVIR = 1536
NOCC_B = 4


def row_weights(pairs, e_occ, e_vir, occ_batch, freq):
    batch_start = occ_batch[0] * NOCC_B
    e_batch = lax.dynamic_slice_in_dim(e_occ, batch_start, NOCC_B, 0)
    occ = pairs // NVIR
    vir = pairs % NVIR
    occ_hit = occ[:, None] == jnp.arange(NOCC_B, dtype=jnp.int32)[None, :]
    vir_hit = vir[:, None] == jnp.arange(e_vir.shape[0], dtype=jnp.int32)[None, :]
    e_low = jnp.sum(jnp.where(occ_hit, e_batch[None, :], 0.0), axis=1)
    e_high = jnp.sum(jnp.where(vir_hit, e_vir[None, :], 0.0), axis=1)
    delta = e_high - e_low
    return 2.0 * delta / (delta * delta + freq[0] * freq[0])


def contract(left, right):
    return lax.dot_general(
        left, right, (((0,), (0,)), ((), ())), preferred_element_type=jnp.float32
    )


def swap(x, axis):
    return lax.ppermute(x, axis, [(0, 1), (1, 0)])


def scale(weight, cols):
    return (weight[:, None] * cols.astype(jnp.float32)).astype(jnp.bfloat16)


def make_body(n_rx, n_rc, n_az, n_ay):
    def body(b_rows, pair_index, e_occ, e_vir, occ_batch, freq):
        nloc, naux = b_rows.shape
        width = naux // (n_az * n_ay)
        rw = naux // (n_rx * n_rc)
        z = lax.axis_index("az")
        x = lax.axis_index("rx")
        c = lax.axis_index("rc")
        a = z * n_ay + lax.axis_index("ay")
        order = [(1 - x) * 2 + (1 - c), x * 2 + (1 - c), (1 - x) * 2 + c, x * 2 + c]
        home = (a * width) // rw
        off = (a * width) % rw

        def others(v):
            doubled = jnp.concatenate([v, v], axis=0)
            return lax.dynamic_slice_in_dim(doubled, (z + 1) * nloc, (n_az - 1) * nloc, axis=0)

        def pick(blocks):
            out = lax.dynamic_slice_in_dim(blocks[0], off, width, axis=1)
            for k in range(1, len(blocks)):
                out = jnp.where(order[k] == home, lax.dynamic_slice_in_dim(blocks[k], off, width, axis=1), out)
            return out

        w_own = row_weights(pair_index, e_occ, e_vir, occ_batch, freq)
        w_z = lax.all_gather(w_own, "az", axis=0, tiled=True)
        first = lax.dynamic_slice_in_dim(b_rows, order[0] * rw, rw, axis=1)
        mine = [lax.all_gather(first, "az", axis=0, tiled=True)]
        w_a = swap(w_own, "ay")
        w_b = swap(others(w_z), "ay")
        theirs_own = swap(b_rows, "ay")
        theirs_own, w_a, w_b, rest = lax.optimization_barrier((theirs_own, w_a, w_b, b_rows))
        theirs = [swap(others(mine[0]), "ay")]
        pieces = []
        for k, m in enumerate(order[1:], start=1):
            parts = 1
            pieces += [(k, m * rw + p * (rw // parts), rw // parts) for p in range(parts)]
        got_mine, got_theirs = [mine[0]], [theirs[0]]
        by_block = {}
        for k, start, pw in pieces:
            _, _, rest = lax.optimization_barrier((got_mine[-1], got_theirs[-2] if len(got_theirs) > 1 else w_a, rest))
            piece = lax.all_gather(lax.dynamic_slice_in_dim(rest, start, pw, axis=1), "az", axis=0, tiled=True)
            got_mine.append(piece)
            got_theirs.append(swap(others(piece), "ay"))
            by_block.setdefault(k, []).append(len(got_mine) - 1)
        for k in range(1, len(order)):
            idx = by_block[k]
            mine.append(jnp.concatenate([got_mine[i] for i in idx], axis=1) if len(idx) > 1 else got_mine[idx[0]])
            theirs.append(jnp.concatenate([got_theirs[i] for i in idx], axis=1) if len(idx) > 1 else got_theirs[idx[0]])
        s_mine = scale(w_z, pick(mine))
        s_a = scale(w_a, lax.dynamic_slice_in_dim(theirs_own, a * width, width, axis=1))
        early = []
        for k, m in enumerate(order):
            cols_a = lax.dynamic_slice_in_dim(theirs_own, m * rw, rw, axis=1)
            early.append(contract(s_a, cols_a) + contract(s_mine, mine[k]))
        s_b = scale(w_b, pick(theirs))
        halves = 2 if width % 16 == 0 else 1
        hw = width // halves
        cuts = [slice(h * hw, (h + 1) * hw) for h in range(halves)]
        sent, got_x = [], []
        for rows in cuts:
            s_h = s_b[:, rows]
            give = early[0][rows] + contract(s_h, theirs[0])
            got = swap(give.astype(jnp.bfloat16), "rc").astype(jnp.float32)
            other_x = early[2][rows] + contract(s_h, theirs[2]) + got
            sent.append(other_x.astype(jnp.bfloat16))
            got_x.append(swap(sent[-1], "rx"))
        _, late_give, late_keep, t_give, t_keep = lax.optimization_barrier(
            (tuple(sent), early[1], early[3], theirs[1], theirs[3])
        )
        out = jnp.zeros((width, rw), jnp.float32)
        for h, rows in enumerate(cuts):
            s_h = s_b[:, rows]
            give = late_give[rows] + contract(s_h, t_give)
            own_x = late_keep[rows] + contract(s_h, t_keep) + swap(give, "rc")
            out = lax.dynamic_update_slice_in_dim(out, own_x + got_x[h].astype(jnp.float32), h * hw, axis=0)
        return out

    return body


def make_plain_body(n_rows, n_aux):
    def body(b_rows, pair_index, e_occ, e_vir, occ_batch, freq):
        width = b_rows.shape[1] // n_aux
        group_pairs = lax.all_gather(pair_index, "aux", axis=0, tiled=True)
        group = lax.all_gather(b_rows, "aux", axis=0, tiled=True)
        own = lax.dynamic_slice_in_dim(group, lax.axis_index("aux") * width, width, axis=1)
        scaled = scale(row_weights(group_pairs, e_occ, e_vir, occ_batch, freq), own)
        return lax.psum_scatter(contract(scaled, group), "rows", scatter_dimension=1, tiled=True)

    return body


def solution(mesh):
    n_rows = mesh.shape["rows"]
    n_aux = mesh.shape["aux"]
    naux = 8192
    fits = n_rows == 4 and n_aux % 2 == 0 and (naux // n_rows) % (naux // n_aux) == 0
    if not fits:
        placed = (P(("rows", "aux"), None), P(("rows", "aux")), P(), P(), P(), P())
        return jax.shard_map(
            make_plain_body(n_rows, n_aux), mesh=mesh, in_specs=placed,
            out_specs=P("aux", "rows"), check_vma=False,
        )
    n_rx, n_rc, n_ay = 2, 2, 2
    n_az = n_aux // n_ay
    split = Mesh(mesh.devices.reshape(n_rx, n_rc, n_az, n_ay), ("rx", "rc", "az", "ay"))
    rows_all = ("rx", "rc", "az", "ay")
    placed = (P(rows_all, None), P(rows_all), P(), P(), P(), P())
    return jax.shard_map(
        make_body(n_rx, n_rc, n_az, n_ay),
        mesh=split,
        in_specs=placed,
        out_specs=P(("az", "ay"), ("rx", "rc")),
        check_vma=False,
    )
```

```python
import jax
import jax.numpy as jnp
from jax import lax
from jax.sharding import Mesh, PartitionSpec as P

NVIR = 1536
NOCC_B = 4


def row_weights(pairs, e_occ, e_vir, occ_batch, freq):
    batch_start = occ_batch[0] * NOCC_B
    e_batch = lax.dynamic_slice_in_dim(e_occ, batch_start, NOCC_B, 0)
    occ = pairs // NVIR
    vir = pairs % NVIR
    occ_hit = occ[:, None] == jnp.arange(NOCC_B, dtype=jnp.int32)[None, :]
    vir_hit = vir[:, None] == jnp.arange(e_vir.shape[0], dtype=jnp.int32)[None, :]
    e_low = jnp.sum(jnp.where(occ_hit, e_batch[None, :], 0.0), axis=1)
    e_high = jnp.sum(jnp.where(vir_hit, e_vir[None, :], 0.0), axis=1)
    delta = e_high - e_low
    return 2.0 * delta / (delta * delta + freq[0] * freq[0])


def contract(left, right):
    return lax.dot_general(
        left, right, (((0,), (0,)), ((), ())), preferred_element_type=jnp.float32
    )


def swap(x, axis):
    return lax.ppermute(x, axis, [(0, 1), (1, 0)])


def scale(weight, cols):
    return (weight[:, None] * cols.astype(jnp.float32)).astype(jnp.bfloat16)


def make_body(n_rx, n_rc, n_az, n_ay):
    def body(b_rows, pair_index, e_occ, e_vir, occ_batch, freq):
        nloc, naux = b_rows.shape
        width = naux // (n_az * n_ay)
        rw = naux // (n_rx * n_rc)
        z = lax.axis_index("az")
        x = lax.axis_index("rx")
        c = lax.axis_index("rc")
        a = z * n_ay + lax.axis_index("ay")
        order = [(1 - x) * 2 + (1 - c), x * 2 + (1 - c), (1 - x) * 2 + c, x * 2 + c]
        home = (a * width) // rw
        off = (a * width) % rw

        def others(v):
            doubled = jnp.concatenate([v, v], axis=0)
            return lax.dynamic_slice_in_dim(doubled, (z + 1) * nloc, (n_az - 1) * nloc, axis=0)

        def pick(blocks):
            out = lax.dynamic_slice_in_dim(blocks[0], off, width, axis=1)
            for k in range(1, len(blocks)):
                out = jnp.where(order[k] == home, lax.dynamic_slice_in_dim(blocks[k], off, width, axis=1), out)
            return out

        w_own = row_weights(pair_index, e_occ, e_vir, occ_batch, freq)
        w_z = lax.all_gather(w_own, "az", axis=0, tiled=True)
        first = lax.dynamic_slice_in_dim(b_rows, order[0] * rw, rw, axis=1)
        mine = [lax.all_gather(first, "az", axis=0, tiled=True)]
        w_a = swap(w_own, "ay")
        w_b = swap(others(w_z), "ay")
        theirs_own = swap(b_rows, "ay")
        theirs_own, w_a, w_b, rest = lax.optimization_barrier((theirs_own, w_a, w_b, b_rows))
        theirs = [swap(others(mine[0]), "ay")]
        pieces = []
        for k, m in enumerate(order[1:], start=1):
            parts = 1
            pieces += [(k, m * rw + p * (rw // parts), rw // parts) for p in range(parts)]
        got_mine, got_theirs = [mine[0]], [theirs[0]]
        by_block = {}
        for k, start, pw in pieces:
            _, _, rest = lax.optimization_barrier((got_mine[-1], got_theirs[-2] if len(got_theirs) > 1 else w_a, rest))
            piece = lax.all_gather(lax.dynamic_slice_in_dim(rest, start, pw, axis=1), "az", axis=0, tiled=True)
            got_mine.append(piece)
            got_theirs.append(swap(others(piece), "ay"))
            by_block.setdefault(k, []).append(len(got_mine) - 1)
        for k in range(1, len(order)):
            idx = by_block[k]
            mine.append(jnp.concatenate([got_mine[i] for i in idx], axis=1) if len(idx) > 1 else got_mine[idx[0]])
            theirs.append(jnp.concatenate([got_theirs[i] for i in idx], axis=1) if len(idx) > 1 else got_theirs[idx[0]])
        s_mine = scale(w_z, pick(mine))
        s_a = scale(w_a, lax.dynamic_slice_in_dim(theirs_own, a * width, width, axis=1))
        early = []
        for k, m in enumerate(order):
            cols_a = lax.dynamic_slice_in_dim(theirs_own, m * rw, rw, axis=1)
            early.append(contract(s_a, cols_a) + contract(s_mine, mine[k]))
        s_b = scale(w_b, pick(theirs))
        halves = 2 if width % 16 == 0 else 1
        hw = width // halves
        cuts = [slice(h * hw, (h + 1) * hw) for h in range(halves)]
        sent, got_x = [], []
        for rows in cuts:
            s_h = s_b[:, rows]
            give = early[0][rows] + contract(s_h, theirs[0])
            got = swap(give.astype(jnp.bfloat16), "rc").astype(jnp.float32)
            other_x = early[2][rows] + contract(s_h, theirs[2]) + got
            sent.append(other_x.astype(jnp.bfloat16))
            got_x.append(swap(sent[-1], "rx"))
        _, late_give, late_keep, t_give, t_keep = lax.optimization_barrier(
            (tuple(sent), early[1], early[3], theirs[1], theirs[3])
        )
        out = jnp.zeros((width, rw), jnp.float32)
        for h, rows in enumerate(cuts):
            s_h = s_b[:, rows]
            give = late_give[rows] + contract(s_h, t_give)
            own_x = late_keep[rows] + contract(s_h, t_keep) + swap(give, "rc")
            out = lax.dynamic_update_slice_in_dim(out, own_x + got_x[h].astype(jnp.float32), h * hw, axis=0)
            if h < halves - 1:
                out = lax.optimization_barrier(out)
        return out

    return body


def make_plain_body(n_rows, n_aux):
    def body(b_rows, pair_index, e_occ, e_vir, occ_batch, freq):
        width = b_rows.shape[1] // n_aux
        group_pairs = lax.all_gather(pair_index, "aux", axis=0, tiled=True)
        group = lax.all_gather(b_rows, "aux", axis=0, tiled=True)
        own = lax.dynamic_slice_in_dim(group, lax.axis_index("aux") * width, width, axis=1)
        scaled = scale(row_weights(group_pairs, e_occ, e_vir, occ_batch, freq), own)
        return lax.psum_scatter(contract(scaled, group), "rows", scatter_dimension=1, tiled=True)

    return body


def solution(mesh):
    n_rows = mesh.shape["rows"]
    n_aux = mesh.shape["aux"]
    naux = 8192
    fits = n_rows == 4 and n_aux % 2 == 0 and (naux // n_rows) % (naux // n_aux) == 0
    if not fits:
        placed = (P(("rows", "aux"), None), P(("rows", "aux")), P(), P(), P(), P())
        return jax.shard_map(
            make_plain_body(n_rows, n_aux), mesh=mesh, in_specs=placed,
            out_specs=P("aux", "rows"), check_vma=False,
        )
    n_rx, n_rc, n_ay = 2, 2, 2
    n_az = n_aux // n_ay
    split = Mesh(mesh.devices.reshape(n_rx, n_rc, n_az, n_ay), ("rx", "rc", "az", "ay"))
    rows_all = ("rx", "rc", "az", "ay")
    placed = (P(rows_all, None), P(rows_all), P(), P(), P(), P())
    return jax.shard_map(
        make_body(n_rx, n_rc, n_az, n_ay),
        mesh=split,
        in_specs=placed,
        out_specs=P(("az", "ay"), ("rx", "rc")),
        check_vma=False,
    )
```

```python
import jax
import jax.numpy as jnp
from jax import lax
from jax.sharding import Mesh, PartitionSpec as P

NVIR = 1536
NOCC_B = 4


def row_weights(pairs, e_occ, e_vir, occ_batch, freq):
    batch_start = occ_batch[0] * NOCC_B
    e_batch = lax.dynamic_slice_in_dim(e_occ, batch_start, NOCC_B, 0)
    occ = pairs // NVIR
    vir = pairs % NVIR
    occ_hit = occ[:, None] == jnp.arange(NOCC_B, dtype=jnp.int32)[None, :]
    vir_hit = vir[:, None] == jnp.arange(e_vir.shape[0], dtype=jnp.int32)[None, :]
    e_low = jnp.sum(jnp.where(occ_hit, e_batch[None, :], 0.0), axis=1)
    e_high = jnp.sum(jnp.where(vir_hit, e_vir[None, :], 0.0), axis=1)
    delta = e_high - e_low
    return 2.0 * delta / (delta * delta + freq[0] * freq[0])


def contract(left, right):
    return lax.dot_general(
        left, right, (((0,), (0,)), ((), ())), preferred_element_type=jnp.float32
    )


def swap(x, axis):
    return lax.ppermute(x, axis, [(0, 1), (1, 0)])


def scale(weight, cols):
    return (weight[:, None] * cols.astype(jnp.float32)).astype(jnp.bfloat16)


def make_body(n_rx, n_rc, n_az, n_ay):
    def body(b_rows, pair_index, e_occ, e_vir, occ_batch, freq):
        nloc, naux = b_rows.shape
        width = naux // (n_az * n_ay)
        rw = naux // (n_rx * n_rc)
        z = lax.axis_index("az")
        x = lax.axis_index("rx")
        c = lax.axis_index("rc")
        a = z * n_ay + lax.axis_index("ay")
        order = [(1 - x) * 2 + (1 - c), (1 - x) * 2 + c, x * 2 + (1 - c), x * 2 + c]
        y = lax.axis_index("ay")

        def others(v):
            doubled = jnp.concatenate([v, v], axis=0)
            return lax.dynamic_slice_in_dim(doubled, (z + 1) * nloc, (n_az - 1) * nloc, axis=0)

        first = lax.dynamic_slice_in_dim(b_rows, order[0] * rw, rw, axis=1)
        mine = [lax.all_gather(first, "az", axis=0, tiled=True)]
        theirs_own = swap(b_rows, "ay")
        w_own = row_weights(pair_index, e_occ, e_vir, occ_batch, freq)
        scaled_rows = lax.all_to_all(scale(w_own, b_rows), ("az", "ay"), 1, 0, tiled=True)
        theirs_own, scaled_rows, rest = lax.optimization_barrier((theirs_own, scaled_rows, b_rows))
        theirs = [swap(others(mine[0]), "ay")]
        for m in order[1:]:
            _, _, rest = lax.optimization_barrier((mine[-1], theirs[-2] if len(theirs) > 1 else theirs_own, rest))
            piece = lax.all_gather(lax.dynamic_slice_in_dim(rest, m * rw, rw, axis=1), "az", axis=0, tiled=True)
            mine.append(piece)
            theirs.append(swap(others(piece), "ay"))
        by_source = scaled_rows.reshape(n_az, n_ay, nloc, width)
        s_mine = lax.dynamic_index_in_dim(by_source, y, axis=1, keepdims=False).reshape(n_az * nloc, width)
        s_other = lax.dynamic_index_in_dim(by_source, 1 - y, axis=1, keepdims=False).reshape(n_az * nloc, width)
        s_a = lax.dynamic_slice_in_dim(s_other, z * nloc, nloc, axis=0)
        s_b = others(s_other)
        early = []
        for k, m in enumerate(order):
            cols_a = lax.dynamic_slice_in_dim(theirs_own, m * rw, rw, axis=1)
            early.append(contract(s_a, cols_a) + contract(s_mine, mine[k]))
        halves = 2 if width % 16 == 0 else 1
        hw = width // halves
        cuts = [slice(h * hw, (h + 1) * hw) for h in range(halves)]
        sent, got_x = [], []
        for rows in cuts:
            s_h = s_b[:, rows]
            give = early[0][rows] + contract(s_h, theirs[0])
            got = swap(give.astype(jnp.bfloat16), "rc").astype(jnp.float32)
            other_x = early[1][rows] + contract(s_h, theirs[1]) + got
            sent.append(other_x.astype(jnp.bfloat16))
            got_x.append(swap(sent[-1], "rx"))
        _, late_give, late_keep, t_give, t_keep = lax.optimization_barrier(
            (tuple(sent), early[2], early[3], theirs[2], theirs[3])
        )
        out = jnp.zeros((width, rw), jnp.float32)
        for h, rows in enumerate(cuts):
            s_h = s_b[:, rows]
            give = late_give[rows] + contract(s_h, t_give)
            own_x = late_keep[rows] + contract(s_h, t_keep) + swap(give, "rc")
            out = lax.dynamic_update_slice_in_dim(out, own_x + got_x[h].astype(jnp.float32), h * hw, axis=0)
            if h < halves - 1:
                out = lax.optimization_barrier(out)
        return out

    return body


def make_plain_body(n_rows, n_aux):
    def body(b_rows, pair_index, e_occ, e_vir, occ_batch, freq):
        width = b_rows.shape[1] // n_aux
        group_pairs = lax.all_gather(pair_index, "aux", axis=0, tiled=True)
        group = lax.all_gather(b_rows, "aux", axis=0, tiled=True)
        own = lax.dynamic_slice_in_dim(group, lax.axis_index("aux") * width, width, axis=1)
        scaled = scale(row_weights(group_pairs, e_occ, e_vir, occ_batch, freq), own)
        return lax.psum_scatter(contract(scaled, group), "rows", scatter_dimension=1, tiled=True)

    return body


def solution(mesh):
    n_rows = mesh.shape["rows"]
    n_aux = mesh.shape["aux"]
    naux = 8192
    fits = n_rows == 4 and n_aux % 2 == 0 and (naux // n_rows) % (naux // n_aux) == 0
    if not fits:
        placed = (P(("rows", "aux"), None), P(("rows", "aux")), P(), P(), P(), P())
        return jax.shard_map(
            make_plain_body(n_rows, n_aux), mesh=mesh, in_specs=placed,
            out_specs=P("aux", "rows"), check_vma=False,
        )
    n_rx, n_rc, n_ay = 2, 2, 2
    n_az = n_aux // n_ay
    split = Mesh(mesh.devices.reshape(n_rx, n_rc, n_az, n_ay), ("rx", "rc", "az", "ay"))
    rows_all = ("rx", "rc", "az", "ay")
    placed = (P(rows_all, None), P(rows_all), P(), P(), P(), P())
    return jax.shard_map(
        make_body(n_rx, n_rc, n_az, n_ay),
        mesh=split,
        in_specs=placed,
        out_specs=P(("az", "ay"), ("rx", "rc")),
        check_vma=False,
    )
```

```python
import jax
import jax.numpy as jnp
from jax import lax
from jax.sharding import Mesh, PartitionSpec as P

NVIR = 1536
NOCC_B = 4


def row_weights(pairs, e_occ, e_vir, occ_batch, freq):
    batch_start = occ_batch[0] * NOCC_B
    e_batch = lax.dynamic_slice_in_dim(e_occ, batch_start, NOCC_B, 0)
    occ = pairs // NVIR
    vir = pairs % NVIR
    occ_hit = occ[:, None] == jnp.arange(NOCC_B, dtype=jnp.int32)[None, :]
    vir_hit = vir[:, None] == jnp.arange(e_vir.shape[0], dtype=jnp.int32)[None, :]
    e_low = jnp.sum(jnp.where(occ_hit, e_batch[None, :], 0.0), axis=1)
    e_high = jnp.sum(jnp.where(vir_hit, e_vir[None, :], 0.0), axis=1)
    delta = e_high - e_low
    return 2.0 * delta / (delta * delta + freq[0] * freq[0])


def contract(left, right):
    return lax.dot_general(
        left, right, (((0,), (0,)), ((), ())), preferred_element_type=jnp.float32
    )


def swap(x, axis):
    return lax.ppermute(x, axis, [(0, 1), (1, 0)])


def scale(weight, cols):
    return (weight[:, None] * cols.astype(jnp.float32)).astype(jnp.bfloat16)


def make_body(n_rx, n_rc, n_az, n_ay):
    def body(b_rows, pair_index, e_occ, e_vir, occ_batch, freq):
        nloc, naux = b_rows.shape
        width = naux // (n_az * n_ay)
        rw = naux // (n_rx * n_rc)
        z = lax.axis_index("az")
        x = lax.axis_index("rx")
        c = lax.axis_index("rc")
        a = z * n_ay + lax.axis_index("ay")
        order = [(1 - x) * 2 + (1 - c), (1 - x) * 2 + c, x * 2 + (1 - c), x * 2 + c]
        y = lax.axis_index("ay")

        def others(v):
            doubled = jnp.concatenate([v, v], axis=0)
            return lax.dynamic_slice_in_dim(doubled, (z + 1) * nloc, (n_az - 1) * nloc, axis=0)

        first = lax.dynamic_slice_in_dim(b_rows, order[0] * rw, rw, axis=1)
        mine = [lax.all_gather(first, "az", axis=0, tiled=True)]
        theirs_own = swap(b_rows, "ay")
        w_own = row_weights(pair_index, e_occ, e_vir, occ_batch, freq)
        scaled_rows = lax.all_to_all(scale(w_own, b_rows), ("az", "ay"), 1, 0, tiled=True)
        theirs_own, scaled_rows, rest = lax.optimization_barrier((theirs_own, scaled_rows, b_rows))
        def x_chain(theirs):
            by_source = scaled_rows.reshape(n_az, n_ay, nloc, width)
            s_mine = lax.dynamic_index_in_dim(by_source, y, axis=1, keepdims=False).reshape(n_az * nloc, width)
            s_other = lax.dynamic_index_in_dim(by_source, 1 - y, axis=1, keepdims=False).reshape(n_az * nloc, width)
            s_a = lax.dynamic_slice_in_dim(s_other, z * nloc, nloc, axis=0)
            s_b = others(s_other)
            early = []
            for k, m in enumerate(order):
                cols_a = lax.dynamic_slice_in_dim(theirs_own, m * rw, rw, axis=1)
                early.append(contract(s_a, cols_a) + contract(s_mine, mine[k]))
            halves = 2 if width % 16 == 0 else 1
            hw = width // halves
            cuts = [slice(h * hw, (h + 1) * hw) for h in range(halves)]
            sent, got_x = [], []
            for rows in cuts:
                s_h = s_b[:, rows]
                give = early[0][rows] + contract(s_h, theirs[0])
                got = swap(give.astype(jnp.bfloat16), "rc").astype(jnp.float32)
                other_x = early[1][rows] + contract(s_h, theirs[1]) + got
                sent.append(other_x.astype(jnp.bfloat16))
                got_x.append(swap(sent[-1], "rx"))
            return s_a, s_b, early, tuple(sent), tuple(got_x), cuts, hw, halves

        x_out = {}
        theirs = [swap(others(mine[0]), "ay")]
        for m in order[1:]:
            _, _, rest = lax.optimization_barrier((mine[-1], theirs[-2] if len(theirs) > 1 else theirs_own, rest))
            piece = lax.all_gather(lax.dynamic_slice_in_dim(rest, m * rw, rw, axis=1), "az", axis=0, tiled=True)
            mine.append(piece)
            outgoing = others(piece)
            if len(mine) == len(order):
                x_out["v"] = x_chain(theirs)
                outgoing = lax.optimization_barrier((outgoing, x_out["v"][4]))[0]
            theirs.append(swap(outgoing, "ay"))
        s_a, s_b, early_part, sent, got_x, cuts, hw, halves = x_out["v"]
        early = list(early_part)
        _, late_give, late_keep, t_give, t_keep = lax.optimization_barrier(
            (tuple(sent), early[2], early[3], theirs[2], theirs[3])
        )
        out = jnp.zeros((width, rw), jnp.float32)
        for h, rows in enumerate(cuts):
            s_h = s_b[:, rows]
            give = late_give[rows] + contract(s_h, t_give)
            own_x = late_keep[rows] + contract(s_h, t_keep) + swap(give, "rc")
            out = lax.dynamic_update_slice_in_dim(out, own_x + got_x[h].astype(jnp.float32), h * hw, axis=0)
            if h < halves - 1:
                out = lax.optimization_barrier(out)
        return out

    return body


def make_plain_body(n_rows, n_aux):
    def body(b_rows, pair_index, e_occ, e_vir, occ_batch, freq):
        width = b_rows.shape[1] // n_aux
        group_pairs = lax.all_gather(pair_index, "aux", axis=0, tiled=True)
        group = lax.all_gather(b_rows, "aux", axis=0, tiled=True)
        own = lax.dynamic_slice_in_dim(group, lax.axis_index("aux") * width, width, axis=1)
        scaled = scale(row_weights(group_pairs, e_occ, e_vir, occ_batch, freq), own)
        return lax.psum_scatter(contract(scaled, group), "rows", scatter_dimension=1, tiled=True)

    return body


def solution(mesh):
    n_rows = mesh.shape["rows"]
    n_aux = mesh.shape["aux"]
    naux = 8192
    fits = n_rows == 4 and n_aux % 2 == 0 and (naux // n_rows) % (naux // n_aux) == 0
    if not fits:
        placed = (P(("rows", "aux"), None), P(("rows", "aux")), P(), P(), P(), P())
        return jax.shard_map(
            make_plain_body(n_rows, n_aux), mesh=mesh, in_specs=placed,
            out_specs=P("aux", "rows"), check_vma=False,
        )
    n_rx, n_rc, n_ay = 2, 2, 2
    n_az = n_aux // n_ay
    split = Mesh(mesh.devices.reshape(n_rx, n_rc, n_az, n_ay), ("rx", "rc", "az", "ay"))
    rows_all = ("rx", "rc", "az", "ay")
    placed = (P(rows_all, None), P(rows_all), P(), P(), P(), P())
    return jax.shard_map(
        make_body(n_rx, n_rc, n_az, n_ay),
        mesh=split,
        in_specs=placed,
        out_specs=P(("az", "ay"), ("rx", "rc")),
        check_vma=False,
    )
```

```python
import jax
import jax.numpy as jnp
from jax import lax
from jax.sharding import Mesh, PartitionSpec as P

NVIR = 1536
NOCC_B = 4


def row_weights(pairs, e_occ, e_vir, occ_batch, freq):
    batch_start = occ_batch[0] * NOCC_B
    e_batch = lax.dynamic_slice_in_dim(e_occ, batch_start, NOCC_B, 0)
    occ = pairs // NVIR
    vir = pairs % NVIR
    occ_hit = occ[:, None] == jnp.arange(NOCC_B, dtype=jnp.int32)[None, :]
    vir_hit = vir[:, None] == jnp.arange(e_vir.shape[0], dtype=jnp.int32)[None, :]
    e_low = jnp.sum(jnp.where(occ_hit, e_batch[None, :], 0.0), axis=1)
    e_high = jnp.sum(jnp.where(vir_hit, e_vir[None, :], 0.0), axis=1)
    delta = e_high - e_low
    return 2.0 * delta / (delta * delta + freq[0] * freq[0])


def contract(left, right):
    return lax.dot_general(
        left, right, (((0,), (0,)), ((), ())), preferred_element_type=jnp.float32
    )


def swap(x, axis):
    return lax.ppermute(x, axis, [(0, 1), (1, 0)])


def scale(weight, cols):
    return (weight[:, None] * cols.astype(jnp.float32)).astype(jnp.bfloat16)


def make_body(n_rx, n_rc, n_az, n_ay):
    def body(b_rows, pair_index, e_occ, e_vir, occ_batch, freq):
        nloc, naux = b_rows.shape
        width = naux // (n_az * n_ay)
        rw = naux // (n_rx * n_rc)
        z = lax.axis_index("az")
        x = lax.axis_index("rx")
        c = lax.axis_index("rc")
        a = z * n_ay + lax.axis_index("ay")
        order = [(1 - x) * 2 + (1 - c), (1 - x) * 2 + c, x * 2 + (1 - c), x * 2 + c]
        y = lax.axis_index("ay")

        def others(v):
            doubled = jnp.concatenate([v, v], axis=0)
            return lax.dynamic_slice_in_dim(doubled, (z + 1) * nloc, (n_az - 1) * nloc, axis=0)

        first = lax.dynamic_slice_in_dim(b_rows, order[0] * rw, rw, axis=1)
        mine = [lax.all_gather(first, "az", axis=0, tiled=True)]
        theirs_own = swap(b_rows, "ay")
        w_own = row_weights(pair_index, e_occ, e_vir, occ_batch, freq)
        scaled_rows = lax.all_to_all(scale(w_own, b_rows), ("az", "ay"), 1, 0, tiled=True)
        theirs_own, scaled_rows, rest = lax.optimization_barrier((theirs_own, scaled_rows, b_rows))
        def x_chain(theirs):
            by_source = scaled_rows.reshape(n_az, n_ay, nloc, width)
            s_mine = lax.dynamic_index_in_dim(by_source, y, axis=1, keepdims=False).reshape(n_az * nloc, width)
            s_other = lax.dynamic_index_in_dim(by_source, 1 - y, axis=1, keepdims=False).reshape(n_az * nloc, width)
            s_a = lax.dynamic_slice_in_dim(s_other, z * nloc, nloc, axis=0)
            s_b = others(s_other)
            early = []
            for k, m in enumerate(order):
                cols_a = lax.dynamic_slice_in_dim(theirs_own, m * rw, rw, axis=1)
                early.append(contract(s_a, cols_a) + contract(s_mine, mine[k]))
            halves = 2 if width % 16 == 0 else 1
            hw = width // halves
            cuts = [slice(h * hw, (h + 1) * hw) for h in range(halves)]
            sent, got_x = [], []
            for rows in cuts:
                s_h = s_b[:, rows]
                give = early[0][rows] + contract(s_h, theirs[0])
                got = swap(give.astype(jnp.bfloat16), "rc").astype(jnp.float32)
                other_x = early[1][rows] + contract(s_h, theirs[1]) + got
                sent.append(other_x.astype(jnp.bfloat16))
                got_x.append(swap(sent[-1], "rx"))
            return s_a, s_b, early, tuple(sent), tuple(got_x), cuts, hw, halves

        x_out = {}
        theirs = [swap(others(mine[0]), "ay")]
        for m in order[1:]:
            _, _, rest = lax.optimization_barrier((mine[-1], theirs[-2] if len(theirs) > 1 else theirs_own, rest))
            piece = lax.all_gather(lax.dynamic_slice_in_dim(rest, m * rw, rw, axis=1), "az", axis=0, tiled=True)
            mine.append(piece)
            outgoing = others(piece)
            if len(mine) == len(order):
                x_out["v"] = x_chain(theirs)
                outgoing = lax.optimization_barrier((outgoing, x_out["v"][4][0]))[0]
            theirs.append(swap(outgoing, "ay"))
        s_a, s_b, early_part, sent, got_x, cuts, hw, halves = x_out["v"]
        early = list(early_part)
        _, late_give, late_keep, t_give, t_keep = lax.optimization_barrier(
            (tuple(sent), early[2], early[3], theirs[2], theirs[3])
        )
        out = jnp.zeros((width, rw), jnp.float32)
        for h, rows in enumerate(cuts):
            s_h = s_b[:, rows]
            give = late_give[rows] + contract(s_h, t_give)
            own_x = late_keep[rows] + contract(s_h, t_keep) + swap(give, "rc")
            out = lax.dynamic_update_slice_in_dim(out, own_x + got_x[h].astype(jnp.float32), h * hw, axis=0)
            if h < halves - 1:
                out = lax.optimization_barrier(out)
        return out

    return body


def make_plain_body(n_rows, n_aux):
    def body(b_rows, pair_index, e_occ, e_vir, occ_batch, freq):
        width = b_rows.shape[1] // n_aux
        group_pairs = lax.all_gather(pair_index, "aux", axis=0, tiled=True)
        group = lax.all_gather(b_rows, "aux", axis=0, tiled=True)
        own = lax.dynamic_slice_in_dim(group, lax.axis_index("aux") * width, width, axis=1)
        scaled = scale(row_weights(group_pairs, e_occ, e_vir, occ_batch, freq), own)
        return lax.psum_scatter(contract(scaled, group), "rows", scatter_dimension=1, tiled=True)

    return body


def solution(mesh):
    n_rows = mesh.shape["rows"]
    n_aux = mesh.shape["aux"]
    naux = 8192
    fits = n_rows == 4 and n_aux % 2 == 0 and (naux // n_rows) % (naux // n_aux) == 0
    if not fits:
        placed = (P(("rows", "aux"), None), P(("rows", "aux")), P(), P(), P(), P())
        return jax.shard_map(
            make_plain_body(n_rows, n_aux), mesh=mesh, in_specs=placed,
            out_specs=P("aux", "rows"), check_vma=False,
        )
    n_rx, n_rc, n_ay = 2, 2, 2
    n_az = n_aux // n_ay
    split = Mesh(mesh.devices.reshape(n_rx, n_rc, n_az, n_ay), ("rx", "rc", "az", "ay"))
    rows_all = ("rx", "rc", "az", "ay")
    placed = (P(rows_all, None), P(rows_all), P(), P(), P(), P())
    return jax.shard_map(
        make_body(n_rx, n_rc, n_az, n_ay),
        mesh=split,
        in_specs=placed,
        out_specs=P(("az", "ay"), ("rx", "rc")),
        check_vma=False,
    )
```

```python
import jax
import jax.numpy as jnp
from jax import lax
from jax.sharding import Mesh, PartitionSpec as P

NVIR = 1536
NOCC_B = 4


def row_weights(pairs, e_occ, e_vir, occ_batch, freq):
    batch_start = occ_batch[0] * NOCC_B
    e_batch = lax.dynamic_slice_in_dim(e_occ, batch_start, NOCC_B, 0)
    occ = pairs // NVIR
    vir = pairs % NVIR
    occ_hit = occ[:, None] == jnp.arange(NOCC_B, dtype=jnp.int32)[None, :]
    vir_hit = vir[:, None] == jnp.arange(e_vir.shape[0], dtype=jnp.int32)[None, :]
    e_low = jnp.sum(jnp.where(occ_hit, e_batch[None, :], 0.0), axis=1)
    e_high = jnp.sum(jnp.where(vir_hit, e_vir[None, :], 0.0), axis=1)
    delta = e_high - e_low
    return 2.0 * delta / (delta * delta + freq[0] * freq[0])


def contract(left, right):
    return lax.dot_general(
        left, right, (((0,), (0,)), ((), ())), preferred_element_type=jnp.float32
    )


def swap(x, axis):
    return lax.ppermute(x, axis, [(0, 1), (1, 0)])


def scale(weight, cols):
    return (weight[:, None] * cols.astype(jnp.float32)).astype(jnp.bfloat16)


def make_body(n_rx, n_rc, n_az, n_ay):
    def body(b_rows, pair_index, e_occ, e_vir, occ_batch, freq):
        nloc, naux = b_rows.shape
        width = naux // (n_az * n_ay)
        rw = naux // (n_rx * n_rc)
        z = lax.axis_index("az")
        x = lax.axis_index("rx")
        c = lax.axis_index("rc")
        a = z * n_ay + lax.axis_index("ay")
        order = [(1 - x) * 2 + (1 - c), (1 - x) * 2 + c, x * 2 + (1 - c), x * 2 + c]
        y = lax.axis_index("ay")

        def others(v):
            doubled = jnp.concatenate([v, v], axis=0)
            return lax.dynamic_slice_in_dim(doubled, (z + 1) * nloc, (n_az - 1) * nloc, axis=0)

        first = lax.dynamic_slice_in_dim(b_rows, order[0] * rw, rw, axis=1)
        mine = [lax.all_gather(first, "az", axis=0, tiled=True)]
        theirs_own = swap(b_rows, "ay")
        w_own = row_weights(pair_index, e_occ, e_vir, occ_batch, freq)
        scaled_rows = lax.all_to_all(scale(w_own, b_rows), ("az", "ay"), 1, 0, tiled=True)
        theirs_own, scaled_rows, rest = lax.optimization_barrier((theirs_own, scaled_rows, b_rows))
        def x_chain(theirs):
            by_source = scaled_rows.reshape(n_az, n_ay, nloc, width)
            s_mine = lax.dynamic_index_in_dim(by_source, y, axis=1, keepdims=False).reshape(n_az * nloc, width)
            s_other = lax.dynamic_index_in_dim(by_source, 1 - y, axis=1, keepdims=False).reshape(n_az * nloc, width)
            s_a = lax.dynamic_slice_in_dim(s_other, z * nloc, nloc, axis=0)
            s_b = others(s_other)
            early = []
            for k, m in enumerate(order):
                cols_a = lax.dynamic_slice_in_dim(theirs_own, m * rw, rw, axis=1)
                early.append(contract(s_a, cols_a) + contract(s_mine, mine[k]))
            halves = 2 if width % 16 == 0 else 1
            hw = width // halves
            cuts = [slice(h * hw, (h + 1) * hw) for h in range(halves)]
            sent, got_x = [], []
            for rows in cuts:
                s_h = s_b[:, rows]
                give = early[0][rows] + contract(s_h, theirs[0])
                got = swap(give.astype(jnp.bfloat16), "rc").astype(jnp.float32)
                other_x = early[1][rows] + contract(s_h, theirs[1]) + got
                sent.append(other_x.astype(jnp.bfloat16))
                got_x.append(swap(sent[-1], "rx"))
            return s_a, s_b, early, tuple(sent), tuple(got_x), cuts, hw, halves

        x_out = {}
        theirs = [swap(others(mine[0]), "ay")]
        for m in order[1:]:
            _, _, rest = lax.optimization_barrier((mine[-1], theirs[-2] if len(theirs) > 1 else theirs_own, rest))
            piece = lax.all_gather(lax.dynamic_slice_in_dim(rest, m * rw, rw, axis=1), "az", axis=0, tiled=True)
            mine.append(piece)
            outgoing = others(piece)
            if len(mine) == len(order) and outgoing.shape[0] % 16 == 0:
                x_out["v"] = x_chain(theirs)
                split_at = outgoing.shape[0] // 2
                head = swap(outgoing[:split_at], "ay")
                tail = lax.optimization_barrier((outgoing[split_at:], x_out["v"][4]))[0]
                theirs.append(jnp.concatenate([head, swap(tail, "ay")], axis=0))
                continue
            if len(mine) == len(order):
                x_out["v"] = x_chain(theirs)
                outgoing = lax.optimization_barrier((outgoing, x_out["v"][4]))[0]
            theirs.append(swap(outgoing, "ay"))
        s_a, s_b, early_part, sent, got_x, cuts, hw, halves = x_out["v"]
        early = list(early_part)
        _, late_give, late_keep, t_give, t_keep = lax.optimization_barrier(
            (tuple(sent), early[2], early[3], theirs[2], theirs[3])
        )
        out = jnp.zeros((width, rw), jnp.float32)
        for h, rows in enumerate(cuts):
            s_h = s_b[:, rows]
            give = late_give[rows] + contract(s_h, t_give)
            own_x = late_keep[rows] + contract(s_h, t_keep) + swap(give, "rc")
            out = lax.dynamic_update_slice_in_dim(out, own_x + got_x[h].astype(jnp.float32), h * hw, axis=0)
            if h < halves - 1:
                out = lax.optimization_barrier(out)
        return out

    return body


def make_plain_body(n_rows, n_aux):
    def body(b_rows, pair_index, e_occ, e_vir, occ_batch, freq):
        width = b_rows.shape[1] // n_aux
        group_pairs = lax.all_gather(pair_index, "aux", axis=0, tiled=True)
        group = lax.all_gather(b_rows, "aux", axis=0, tiled=True)
        own = lax.dynamic_slice_in_dim(group, lax.axis_index("aux") * width, width, axis=1)
        scaled = scale(row_weights(group_pairs, e_occ, e_vir, occ_batch, freq), own)
        return lax.psum_scatter(contract(scaled, group), "rows", scatter_dimension=1, tiled=True)

    return body


def solution(mesh):
    n_rows = mesh.shape["rows"]
    n_aux = mesh.shape["aux"]
    naux = 8192
    fits = n_rows == 4 and n_aux % 2 == 0 and (naux // n_rows) % (naux // n_aux) == 0
    if not fits:
        placed = (P(("rows", "aux"), None), P(("rows", "aux")), P(), P(), P(), P())
        return jax.shard_map(
            make_plain_body(n_rows, n_aux), mesh=mesh, in_specs=placed,
            out_specs=P("aux", "rows"), check_vma=False,
        )
    n_rx, n_rc, n_ay = 2, 2, 2
    n_az = n_aux // n_ay
    split = Mesh(mesh.devices.reshape(n_rx, n_rc, n_az, n_ay), ("rx", "rc", "az", "ay"))
    rows_all = ("rx", "rc", "az", "ay")
    placed = (P(rows_all, None), P(rows_all), P(), P(), P(), P())
    return jax.shard_map(
        make_body(n_rx, n_rc, n_az, n_ay),
        mesh=split,
        in_specs=placed,
        out_specs=P(("az", "ay"), ("rx", "rc")),
        check_vma=False,
    )
```

```python
import jax
import jax.numpy as jnp
from jax import lax
from jax.sharding import Mesh, PartitionSpec as P

NVIR = 1536
NOCC_B = 4


def row_weights(pairs, e_occ, e_vir, occ_batch, freq):
    batch_start = occ_batch[0] * NOCC_B
    e_batch = lax.dynamic_slice_in_dim(e_occ, batch_start, NOCC_B, 0)
    occ = pairs // NVIR
    vir = pairs % NVIR
    occ_hit = occ[:, None] == jnp.arange(NOCC_B, dtype=jnp.int32)[None, :]
    vir_hit = vir[:, None] == jnp.arange(e_vir.shape[0], dtype=jnp.int32)[None, :]
    e_low = jnp.sum(jnp.where(occ_hit, e_batch[None, :], 0.0), axis=1)
    e_high = jnp.sum(jnp.where(vir_hit, e_vir[None, :], 0.0), axis=1)
    delta = e_high - e_low
    return 2.0 * delta / (delta * delta + freq[0] * freq[0])


def contract(left, right):
    return lax.dot_general(
        left, right, (((0,), (0,)), ((), ())), preferred_element_type=jnp.float32
    )


def swap(x, axis):
    return lax.ppermute(x, axis, [(0, 1), (1, 0)])


def scale(weight, cols):
    return (weight[:, None] * cols.astype(jnp.float32)).astype(jnp.bfloat16)


def make_body(n_rx, n_rc, n_az, n_ay):
    def body(b_rows, pair_index, e_occ, e_vir, occ_batch, freq):
        nloc, naux = b_rows.shape
        width = naux // (n_az * n_ay)
        rw = naux // (n_rx * n_rc)
        z = lax.axis_index("az")
        x = lax.axis_index("rx")
        c = lax.axis_index("rc")
        a = z * n_ay + lax.axis_index("ay")
        order = [(1 - x) * 2 + (1 - c), (1 - x) * 2 + c, x * 2 + (1 - c), x * 2 + c]
        y = lax.axis_index("ay")

        def others(v):
            doubled = jnp.concatenate([v, v], axis=0)
            return lax.dynamic_slice_in_dim(doubled, (z + 1) * nloc, (n_az - 1) * nloc, axis=0)

        first = lax.dynamic_slice_in_dim(b_rows, order[0] * rw, rw, axis=1)
        mine = [lax.all_gather(first, "az", axis=0, tiled=True)]
        theirs_own = swap(b_rows, "ay")
        w_own = row_weights(pair_index, e_occ, e_vir, occ_batch, freq)
        scaled_rows = lax.all_to_all(scale(w_own, b_rows), ("az", "ay"), 1, 0, tiled=True)
        theirs_own, scaled_rows, rest = lax.optimization_barrier((theirs_own, scaled_rows, b_rows))
        def x_chain(theirs):
            by_source = scaled_rows.reshape(n_az, n_ay, nloc, width)
            s_mine = lax.dynamic_index_in_dim(by_source, y, axis=1, keepdims=False).reshape(n_az * nloc, width)
            s_other = lax.dynamic_index_in_dim(by_source, 1 - y, axis=1, keepdims=False).reshape(n_az * nloc, width)
            s_a = lax.dynamic_slice_in_dim(s_other, z * nloc, nloc, axis=0)
            s_b = others(s_other)
            early = []
            for k, m in enumerate(order):
                cols_a = lax.dynamic_slice_in_dim(theirs_own, m * rw, rw, axis=1)
                early.append(contract(s_a, cols_a) + contract(s_mine, mine[k]))
            halves = 1
            hw = width // halves
            cuts = [slice(h * hw, (h + 1) * hw) for h in range(halves)]
            sent, got_x = [], []
            for rows in cuts:
                s_h = s_b[:, rows]
                give = early[0][rows] + contract(s_h, theirs[0])
                got = swap(give.astype(jnp.bfloat16), "rc").astype(jnp.float32)
                other_x = early[1][rows] + contract(s_h, theirs[1]) + got
                sent.append(other_x.astype(jnp.bfloat16))
                got_x.append(swap(sent[-1], "rx"))
            return s_a, s_b, early, tuple(sent), tuple(got_x), cuts, hw, halves

        x_out = {}
        theirs = [swap(others(mine[0]), "ay")]
        for m in order[1:]:
            _, _, rest = lax.optimization_barrier((mine[-1], theirs[-2] if len(theirs) > 1 else theirs_own, rest))
            piece = lax.all_gather(lax.dynamic_slice_in_dim(rest, m * rw, rw, axis=1), "az", axis=0, tiled=True)
            mine.append(piece)
            outgoing = others(piece)
            if len(mine) == len(order):
                x_out["v"] = x_chain(theirs)
                outgoing = lax.optimization_barrier((outgoing, x_out["v"][4]))[0]
            theirs.append(swap(outgoing, "ay"))
        s_a, s_b, early_part, sent, got_x, cuts, hw, halves = x_out["v"]
        early = list(early_part)
        _, late_give, late_keep, t_give, t_keep = lax.optimization_barrier(
            (tuple(sent), early[2], early[3], theirs[2], theirs[3])
        )
        out = jnp.zeros((width, rw), jnp.float32)
        for h, rows in enumerate(cuts):
            s_h = s_b[:, rows]
            give = late_give[rows] + contract(s_h, t_give)
            own_x = late_keep[rows] + contract(s_h, t_keep) + swap(give, "rc")
            out = lax.dynamic_update_slice_in_dim(out, own_x + got_x[h].astype(jnp.float32), h * hw, axis=0)
            if h < halves - 1:
                out = lax.optimization_barrier(out)
        return out

    return body


def make_plain_body(n_rows, n_aux):
    def body(b_rows, pair_index, e_occ, e_vir, occ_batch, freq):
        width = b_rows.shape[1] // n_aux
        group_pairs = lax.all_gather(pair_index, "aux", axis=0, tiled=True)
        group = lax.all_gather(b_rows, "aux", axis=0, tiled=True)
        own = lax.dynamic_slice_in_dim(group, lax.axis_index("aux") * width, width, axis=1)
        scaled = scale(row_weights(group_pairs, e_occ, e_vir, occ_batch, freq), own)
        return lax.psum_scatter(contract(scaled, group), "rows", scatter_dimension=1, tiled=True)

    return body


def solution(mesh):
    n_rows = mesh.shape["rows"]
    n_aux = mesh.shape["aux"]
    naux = 8192
    fits = n_rows == 4 and n_aux % 2 == 0 and (naux // n_rows) % (naux // n_aux) == 0
    if not fits:
        placed = (P(("rows", "aux"), None), P(("rows", "aux")), P(), P(), P(), P())
        return jax.shard_map(
            make_plain_body(n_rows, n_aux), mesh=mesh, in_specs=placed,
            out_specs=P("aux", "rows"), check_vma=False,
        )
    n_rx, n_rc, n_ay = 2, 2, 2
    n_az = n_aux // n_ay
    split = Mesh(mesh.devices.reshape(n_rx, n_rc, n_az, n_ay), ("rx", "rc", "az", "ay"))
    rows_all = ("rx", "rc", "az", "ay")
    placed = (P(rows_all, None), P(rows_all), P(), P(), P(), P())
    return jax.shard_map(
        make_body(n_rx, n_rc, n_az, n_ay),
        mesh=split,
        in_specs=placed,
        out_specs=P(("az", "ay"), ("rx", "rc")),
        check_vma=False,
    )
```

```python
import jax
import jax.numpy as jnp
from jax import lax
from jax.sharding import Mesh, PartitionSpec as P

NVIR = 1536
NOCC_B = 4


def row_weights(pairs, e_occ, e_vir, occ_batch, freq):
    batch_start = occ_batch[0] * NOCC_B
    e_batch = lax.dynamic_slice_in_dim(e_occ, batch_start, NOCC_B, 0)
    occ = pairs // NVIR
    vir = pairs % NVIR
    occ_hit = occ[:, None] == jnp.arange(NOCC_B, dtype=jnp.int32)[None, :]
    vir_hit = vir[:, None] == jnp.arange(e_vir.shape[0], dtype=jnp.int32)[None, :]
    e_low = jnp.sum(jnp.where(occ_hit, e_batch[None, :], 0.0), axis=1)
    e_high = jnp.sum(jnp.where(vir_hit, e_vir[None, :], 0.0), axis=1)
    delta = e_high - e_low
    return 2.0 * delta / (delta * delta + freq[0] * freq[0])


def contract(left, right):
    return lax.dot_general(
        left, right, (((0,), (0,)), ((), ())), preferred_element_type=jnp.float32
    )


def swap(x, axis):
    return lax.ppermute(x, axis, [(0, 1), (1, 0)])


def scale(weight, cols):
    return (weight[:, None] * cols.astype(jnp.float32)).astype(jnp.bfloat16)


def make_body(n_rx, n_rc, n_az, n_ay):
    def body(b_rows, pair_index, e_occ, e_vir, occ_batch, freq):
        nloc, naux = b_rows.shape
        width = naux // (n_az * n_ay)
        rw = naux // (n_rx * n_rc)
        z = lax.axis_index("az")
        x = lax.axis_index("rx")
        c = lax.axis_index("rc")
        a = z * n_ay + lax.axis_index("ay")
        order = [(1 - x) * 2 + (1 - c), (1 - x) * 2 + c, x * 2 + (1 - c), x * 2 + c]
        y = lax.axis_index("ay")

        def others(v):
            doubled = jnp.concatenate([v, v], axis=0)
            return lax.dynamic_slice_in_dim(doubled, (z + 1) * nloc, (n_az - 1) * nloc, axis=0)

        first = lax.dynamic_slice_in_dim(b_rows, order[0] * rw, rw, axis=1)
        mine = [lax.all_gather(first, "az", axis=0, tiled=True)]
        theirs_own = swap(b_rows, "ay")
        w_own = row_weights(pair_index, e_occ, e_vir, occ_batch, freq)
        scaled_rows = lax.all_to_all(scale(w_own, b_rows), ("az", "ay"), 1, 0, tiled=True)
        theirs_own, rest = lax.optimization_barrier((theirs_own, b_rows))
        def x_chain(theirs):
            by_source = scaled_rows.reshape(n_az, n_ay, nloc, width)
            s_mine = lax.dynamic_index_in_dim(by_source, y, axis=1, keepdims=False).reshape(n_az * nloc, width)
            s_other = lax.dynamic_index_in_dim(by_source, 1 - y, axis=1, keepdims=False).reshape(n_az * nloc, width)
            s_a = lax.dynamic_slice_in_dim(s_other, z * nloc, nloc, axis=0)
            s_b = others(s_other)
            early = []
            for k, m in enumerate(order):
                cols_a = lax.dynamic_slice_in_dim(theirs_own, m * rw, rw, axis=1)
                early.append(contract(s_a, cols_a) + contract(s_mine, mine[k]))
            halves = 2 if width % 16 == 0 else 1
            hw = width // halves
            cuts = [slice(h * hw, (h + 1) * hw) for h in range(halves)]
            sent, got_x = [], []
            for rows in cuts:
                s_h = s_b[:, rows]
                give = early[0][rows] + contract(s_h, theirs[0])
                got = swap(give.astype(jnp.bfloat16), "rc").astype(jnp.float32)
                other_x = early[1][rows] + contract(s_h, theirs[1]) + got
                sent.append(other_x.astype(jnp.bfloat16))
                got_x.append(swap(sent[-1], "rx"))
            return s_a, s_b, early, tuple(sent), tuple(got_x), cuts, hw, halves

        x_out = {}
        theirs = [swap(others(mine[0]), "ay")]
        for m in order[1:]:
            _, _, rest = lax.optimization_barrier((mine[-1], theirs[-2] if len(theirs) > 1 else theirs_own, rest))
            piece = lax.all_gather(lax.dynamic_slice_in_dim(rest, m * rw, rw, axis=1), "az", axis=0, tiled=True)
            mine.append(piece)
            outgoing = others(piece)
            if len(mine) == len(order):
                x_out["v"] = x_chain(theirs)
                outgoing = lax.optimization_barrier((outgoing, x_out["v"][4]))[0]
            theirs.append(swap(outgoing, "ay"))
        s_a, s_b, early_part, sent, got_x, cuts, hw, halves = x_out["v"]
        early = list(early_part)
        _, late_give, late_keep, t_give, t_keep = lax.optimization_barrier(
            (tuple(sent), early[2], early[3], theirs[2], theirs[3])
        )
        out = jnp.zeros((width, rw), jnp.float32)
        for h, rows in enumerate(cuts):
            s_h = s_b[:, rows]
            give = late_give[rows] + contract(s_h, t_give)
            own_x = late_keep[rows] + contract(s_h, t_keep) + swap(give, "rc")
            out = lax.dynamic_update_slice_in_dim(out, own_x + got_x[h].astype(jnp.float32), h * hw, axis=0)
            if h < halves - 1:
                out = lax.optimization_barrier(out)
        return out

    return body


def make_plain_body(n_rows, n_aux):
    def body(b_rows, pair_index, e_occ, e_vir, occ_batch, freq):
        width = b_rows.shape[1] // n_aux
        group_pairs = lax.all_gather(pair_index, "aux", axis=0, tiled=True)
        group = lax.all_gather(b_rows, "aux", axis=0, tiled=True)
        own = lax.dynamic_slice_in_dim(group, lax.axis_index("aux") * width, width, axis=1)
        scaled = scale(row_weights(group_pairs, e_occ, e_vir, occ_batch, freq), own)
        return lax.psum_scatter(contract(scaled, group), "rows", scatter_dimension=1, tiled=True)

    return body


def solution(mesh):
    n_rows = mesh.shape["rows"]
    n_aux = mesh.shape["aux"]
    naux = 8192
    fits = n_rows == 4 and n_aux % 2 == 0 and (naux // n_rows) % (naux // n_aux) == 0
    if not fits:
        placed = (P(("rows", "aux"), None), P(("rows", "aux")), P(), P(), P(), P())
        return jax.shard_map(
            make_plain_body(n_rows, n_aux), mesh=mesh, in_specs=placed,
            out_specs=P("aux", "rows"), check_vma=False,
        )
    n_rx, n_rc, n_ay = 2, 2, 2
    n_az = n_aux // n_ay
    split = Mesh(mesh.devices.reshape(n_rx, n_rc, n_az, n_ay), ("rx", "rc", "az", "ay"))
    rows_all = ("rx", "rc", "az", "ay")
    placed = (P(rows_all, None), P(rows_all), P(), P(), P(), P())
    return jax.shard_map(
        make_body(n_rx, n_rc, n_az, n_ay),
        mesh=split,
        in_specs=placed,
        out_specs=P(("az", "ay"), ("rx", "rc")),
        check_vma=False,
    )
```

```python
import jax
import jax.numpy as jnp
from jax import lax
from jax.sharding import Mesh, PartitionSpec as P

NVIR = 1536
NOCC_B = 4


def row_weights(pairs, e_occ, e_vir, occ_batch, freq):
    batch_start = occ_batch[0] * NOCC_B
    e_batch = lax.dynamic_slice_in_dim(e_occ, batch_start, NOCC_B, 0)
    occ = pairs // NVIR
    vir = pairs % NVIR
    occ_hit = occ[:, None] == jnp.arange(NOCC_B, dtype=jnp.int32)[None, :]
    vir_hit = vir[:, None] == jnp.arange(e_vir.shape[0], dtype=jnp.int32)[None, :]
    e_low = jnp.sum(jnp.where(occ_hit, e_batch[None, :], 0.0), axis=1)
    e_high = jnp.sum(jnp.where(vir_hit, e_vir[None, :], 0.0), axis=1)
    delta = e_high - e_low
    return 2.0 * delta / (delta * delta + freq[0] * freq[0])


def contract(left, right):
    return lax.dot_general(
        left, right, (((0,), (0,)), ((), ())), preferred_element_type=jnp.float32
    )


def swap(x, axis):
    return lax.ppermute(x, axis, [(0, 1), (1, 0)])


def scale(weight, cols):
    return (weight[:, None] * cols.astype(jnp.float32)).astype(jnp.bfloat16)


def make_body(n_rx, n_rc, n_az, n_ay):
    def body(b_rows, pair_index, e_occ, e_vir, occ_batch, freq):
        nloc, naux = b_rows.shape
        width = naux // (n_az * n_ay)
        rw = naux // (n_rx * n_rc)
        z = lax.axis_index("az")
        x = lax.axis_index("rx")
        c = lax.axis_index("rc")
        a = z * n_ay + lax.axis_index("ay")
        order = [(1 - x) * 2 + (1 - c), (1 - x) * 2 + c, x * 2 + (1 - c), x * 2 + c]
        y = lax.axis_index("ay")

        def others(v):
            doubled = jnp.concatenate([v, v], axis=0)
            return lax.dynamic_slice_in_dim(doubled, (z + 1) * nloc, (n_az - 1) * nloc, axis=0)

        first = lax.dynamic_slice_in_dim(b_rows, order[0] * rw, rw, axis=1)
        mine = [lax.all_gather(first, "az", axis=0, tiled=True)]
        theirs_own = swap(b_rows, "ay")
        w_own = row_weights(pair_index, e_occ, e_vir, occ_batch, freq)
        scaled_rows = lax.all_to_all(scale(w_own, b_rows), ("az", "ay"), 1, 0, tiled=True)
        theirs_own, rest = lax.optimization_barrier((theirs_own, b_rows))
        def x_chain(theirs):
            by_source = scaled_rows.reshape(n_az, n_ay, nloc, width)
            s_mine = lax.dynamic_index_in_dim(by_source, y, axis=1, keepdims=False).reshape(n_az * nloc, width)
            s_other = lax.dynamic_index_in_dim(by_source, 1 - y, axis=1, keepdims=False).reshape(n_az * nloc, width)
            s_a = lax.dynamic_slice_in_dim(s_other, z * nloc, nloc, axis=0)
            s_b = others(s_other)
            early = []
            for k, m in enumerate(order):
                cols_a = lax.dynamic_slice_in_dim(theirs_own, m * rw, rw, axis=1)
                early.append(contract(s_a, cols_a) + contract(s_mine, mine[k]))
            halves = 4 if width % 32 == 0 else 1
            hw = width // halves
            cuts = [slice(h * hw, (h + 1) * hw) for h in range(halves)]
            sent, got_x = [], []
            for rows in cuts:
                s_h = s_b[:, rows]
                give = early[0][rows] + contract(s_h, theirs[0])
                got = swap(give.astype(jnp.bfloat16), "rc").astype(jnp.float32)
                other_x = early[1][rows] + contract(s_h, theirs[1]) + got
                sent.append(other_x.astype(jnp.bfloat16))
                got_x.append(swap(sent[-1], "rx"))
            return s_a, s_b, early, tuple(sent), tuple(got_x), cuts, hw, halves

        x_out = {}
        theirs = [swap(others(mine[0]), "ay")]
        for m in order[1:]:
            _, _, rest = lax.optimization_barrier((mine[-1], theirs[-2] if len(theirs) > 1 else theirs_own, rest))
            piece = lax.all_gather(lax.dynamic_slice_in_dim(rest, m * rw, rw, axis=1), "az", axis=0, tiled=True)
            mine.append(piece)
            outgoing = others(piece)
            if len(mine) == len(order):
                x_out["v"] = x_chain(theirs)
                outgoing = lax.optimization_barrier((outgoing, x_out["v"][4]))[0]
            theirs.append(swap(outgoing, "ay"))
        s_a, s_b, early_part, sent, got_x, cuts, hw, halves = x_out["v"]
        early = list(early_part)
        _, late_give, late_keep, t_give, t_keep = lax.optimization_barrier(
            (tuple(sent), early[2], early[3], theirs[2], theirs[3])
        )
        out = jnp.zeros((width, rw), jnp.float32)
        for h, rows in enumerate(cuts):
            s_h = s_b[:, rows]
            give = late_give[rows] + contract(s_h, t_give)
            own_x = late_keep[rows] + contract(s_h, t_keep) + swap(give, "rc")
            out = lax.dynamic_update_slice_in_dim(out, own_x + got_x[h].astype(jnp.float32), h * hw, axis=0)
            if h < halves - 1:
                out = lax.optimization_barrier(out)
        return out

    return body


def make_plain_body(n_rows, n_aux):
    def body(b_rows, pair_index, e_occ, e_vir, occ_batch, freq):
        width = b_rows.shape[1] // n_aux
        group_pairs = lax.all_gather(pair_index, "aux", axis=0, tiled=True)
        group = lax.all_gather(b_rows, "aux", axis=0, tiled=True)
        own = lax.dynamic_slice_in_dim(group, lax.axis_index("aux") * width, width, axis=1)
        scaled = scale(row_weights(group_pairs, e_occ, e_vir, occ_batch, freq), own)
        return lax.psum_scatter(contract(scaled, group), "rows", scatter_dimension=1, tiled=True)

    return body


def solution(mesh):
    n_rows = mesh.shape["rows"]
    n_aux = mesh.shape["aux"]
    naux = 8192
    fits = n_rows == 4 and n_aux % 2 == 0 and (naux // n_rows) % (naux // n_aux) == 0
    if not fits:
        placed = (P(("rows", "aux"), None), P(("rows", "aux")), P(), P(), P(), P())
        return jax.shard_map(
            make_plain_body(n_rows, n_aux), mesh=mesh, in_specs=placed,
            out_specs=P("aux", "rows"), check_vma=False,
        )
    n_rx, n_rc, n_ay = 2, 2, 2
    n_az = n_aux // n_ay
    split = Mesh(mesh.devices.reshape(n_rx, n_rc, n_az, n_ay), ("rx", "rc", "az", "ay"))
    rows_all = ("rx", "rc", "az", "ay")
    placed = (P(rows_all, None), P(rows_all), P(), P(), P(), P())
    return jax.shard_map(
        make_body(n_rx, n_rc, n_az, n_ay),
        mesh=split,
        in_specs=placed,
        out_specs=P(("az", "ay"), ("rx", "rc")),
        check_vma=False,
    )
```

```python
import jax
import jax.numpy as jnp
from jax import lax
from jax.sharding import Mesh, PartitionSpec as P

NVIR = 1536
NOCC_B = 4


def row_weights(pairs, e_occ, e_vir, occ_batch, freq):
    batch_start = occ_batch[0] * NOCC_B
    e_batch = lax.dynamic_slice_in_dim(e_occ, batch_start, NOCC_B, 0)
    occ = pairs // NVIR
    vir = pairs % NVIR
    occ_hit = occ[:, None] == jnp.arange(NOCC_B, dtype=jnp.int32)[None, :]
    vir_hit = vir[:, None] == jnp.arange(e_vir.shape[0], dtype=jnp.int32)[None, :]
    e_low = jnp.sum(jnp.where(occ_hit, e_batch[None, :], 0.0), axis=1)
    e_high = jnp.sum(jnp.where(vir_hit, e_vir[None, :], 0.0), axis=1)
    delta = e_high - e_low
    return 2.0 * delta / (delta * delta + freq[0] * freq[0])


def contract(left, right):
    return lax.dot_general(
        left, right, (((0,), (0,)), ((), ())), preferred_element_type=jnp.float32
    )


def swap(x, axis):
    return lax.ppermute(x, axis, [(0, 1), (1, 0)])


def scale(weight, cols):
    return (weight[:, None] * cols.astype(jnp.float32)).astype(jnp.bfloat16)


def make_body(n_rx, n_rc, n_az, n_ay):
    def body(b_rows, pair_index, e_occ, e_vir, occ_batch, freq):
        nloc, naux = b_rows.shape
        width = naux // (n_az * n_ay)
        rw = naux // (n_rx * n_rc)
        z = lax.axis_index("az")
        x = lax.axis_index("rx")
        c = lax.axis_index("rc")
        a = z * n_ay + lax.axis_index("ay")
        order = [(1 - x) * 2 + (1 - c), (1 - x) * 2 + c, x * 2 + (1 - c), x * 2 + c]
        y = lax.axis_index("ay")

        def others(v):
            doubled = jnp.concatenate([v, v], axis=0)
            return lax.dynamic_slice_in_dim(doubled, (z + 1) * nloc, (n_az - 1) * nloc, axis=0)

        first = lax.dynamic_slice_in_dim(b_rows, order[0] * rw, rw, axis=1)
        mine = [lax.all_gather(first, "az", axis=0, tiled=True)]
        theirs_own = swap(b_rows, "ay")
        w_own = row_weights(pair_index, e_occ, e_vir, occ_batch, freq)
        scaled_rows = lax.all_to_all(scale(w_own, b_rows), ("az", "ay"), 1, 0, tiled=True)
        theirs_own, rest = lax.optimization_barrier((theirs_own, b_rows))
        def x_chain(theirs):
            by_source = scaled_rows.reshape(n_az, n_ay, nloc, width)
            s_mine = lax.dynamic_index_in_dim(by_source, y, axis=1, keepdims=False).reshape(n_az * nloc, width)
            s_other = lax.dynamic_index_in_dim(by_source, 1 - y, axis=1, keepdims=False).reshape(n_az * nloc, width)
            s_a = lax.dynamic_slice_in_dim(s_other, z * nloc, nloc, axis=0)
            s_b = others(s_other)
            early = []
            for k, m in enumerate(order):
                cols_a = lax.dynamic_slice_in_dim(theirs_own, m * rw, rw, axis=1)
                early.append(contract(s_a, cols_a) + contract(s_mine, mine[k]))
            halves = 8 if width % 64 == 0 else 1
            hw = width // halves
            cuts = [slice(h * hw, (h + 1) * hw) for h in range(halves)]
            sent, got_x = [], []
            for rows in cuts:
                s_h = s_b[:, rows]
                give = early[0][rows] + contract(s_h, theirs[0])
                got = swap(give.astype(jnp.bfloat16), "rc").astype(jnp.float32)
                other_x = early[1][rows] + contract(s_h, theirs[1]) + got
                sent.append(other_x.astype(jnp.bfloat16))
                got_x.append(swap(sent[-1], "rx"))
            return s_a, s_b, early, tuple(sent), tuple(got_x), cuts, hw, halves

        x_out = {}
        theirs = [swap(others(mine[0]), "ay")]
        for m in order[1:]:
            _, _, rest = lax.optimization_barrier((mine[-1], theirs[-2] if len(theirs) > 1 else theirs_own, rest))
            piece = lax.all_gather(lax.dynamic_slice_in_dim(rest, m * rw, rw, axis=1), "az", axis=0, tiled=True)
            mine.append(piece)
            outgoing = others(piece)
            if len(mine) == len(order):
                x_out["v"] = x_chain(theirs)
                outgoing = lax.optimization_barrier((outgoing, x_out["v"][4]))[0]
            theirs.append(swap(outgoing, "ay"))
        s_a, s_b, early_part, sent, got_x, cuts, hw, halves = x_out["v"]
        early = list(early_part)
        _, late_give, late_keep, t_give, t_keep = lax.optimization_barrier(
            (tuple(sent), early[2], early[3], theirs[2], theirs[3])
        )
        out = jnp.zeros((width, rw), jnp.float32)
        for h, rows in enumerate(cuts):
            s_h = s_b[:, rows]
            give = late_give[rows] + contract(s_h, t_give)
            own_x = late_keep[rows] + contract(s_h, t_keep) + swap(give, "rc")
            out = lax.dynamic_update_slice_in_dim(out, own_x + got_x[h].astype(jnp.float32), h * hw, axis=0)
            if h < halves - 1:
                out = lax.optimization_barrier(out)
        return out

    return body


def make_plain_body(n_rows, n_aux):
    def body(b_rows, pair_index, e_occ, e_vir, occ_batch, freq):
        width = b_rows.shape[1] // n_aux
        group_pairs = lax.all_gather(pair_index, "aux", axis=0, tiled=True)
        group = lax.all_gather(b_rows, "aux", axis=0, tiled=True)
        own = lax.dynamic_slice_in_dim(group, lax.axis_index("aux") * width, width, axis=1)
        scaled = scale(row_weights(group_pairs, e_occ, e_vir, occ_batch, freq), own)
        return lax.psum_scatter(contract(scaled, group), "rows", scatter_dimension=1, tiled=True)

    return body


def solution(mesh):
    n_rows = mesh.shape["rows"]
    n_aux = mesh.shape["aux"]
    naux = 8192
    fits = n_rows == 4 and n_aux % 2 == 0 and (naux // n_rows) % (naux // n_aux) == 0
    if not fits:
        placed = (P(("rows", "aux"), None), P(("rows", "aux")), P(), P(), P(), P())
        return jax.shard_map(
            make_plain_body(n_rows, n_aux), mesh=mesh, in_specs=placed,
            out_specs=P("aux", "rows"), check_vma=False,
        )
    n_rx, n_rc, n_ay = 2, 2, 2
    n_az = n_aux // n_ay
    split = Mesh(mesh.devices.reshape(n_rx, n_rc, n_az, n_ay), ("rx", "rc", "az", "ay"))
    rows_all = ("rx", "rc", "az", "ay")
    placed = (P(rows_all, None), P(rows_all), P(), P(), P(), P())
    return jax.shard_map(
        make_body(n_rx, n_rc, n_az, n_ay),
        mesh=split,
        in_specs=placed,
        out_specs=P(("az", "ay"), ("rx", "rc")),
        check_vma=False,
    )
```

```python
import jax
import jax.numpy as jnp
from jax import lax
from jax.sharding import Mesh, PartitionSpec as P

NVIR = 1536
NOCC_B = 4


def row_weights(pairs, e_occ, e_vir, occ_batch, freq):
    batch_start = occ_batch[0] * NOCC_B
    e_batch = lax.dynamic_slice_in_dim(e_occ, batch_start, NOCC_B, 0)
    occ = pairs // NVIR
    vir = pairs % NVIR
    occ_hit = occ[:, None] == jnp.arange(NOCC_B, dtype=jnp.int32)[None, :]
    vir_hit = vir[:, None] == jnp.arange(e_vir.shape[0], dtype=jnp.int32)[None, :]
    e_low = jnp.sum(jnp.where(occ_hit, e_batch[None, :], 0.0), axis=1)
    e_high = jnp.sum(jnp.where(vir_hit, e_vir[None, :], 0.0), axis=1)
    delta = e_high - e_low
    return 2.0 * delta / (delta * delta + freq[0] * freq[0])


def contract(left, right):
    return lax.dot_general(
        left, right, (((0,), (0,)), ((), ())), preferred_element_type=jnp.float32
    )


def swap(x, axis):
    return lax.ppermute(x, axis, [(0, 1), (1, 0)])


def scale(weight, cols):
    return (weight[:, None] * cols.astype(jnp.float32)).astype(jnp.bfloat16)


def make_body(n_rx, n_rc, n_az, n_ay):
    def body(b_rows, pair_index, e_occ, e_vir, occ_batch, freq):
        nloc, naux = b_rows.shape
        width = naux // (n_az * n_ay)
        rw = naux // (n_rx * n_rc)
        z = lax.axis_index("az")
        x = lax.axis_index("rx")
        c = lax.axis_index("rc")
        a = z * n_ay + lax.axis_index("ay")
        order = [(1 - x) * 2 + (1 - c), (1 - x) * 2 + c, x * 2 + (1 - c), x * 2 + c]
        y = lax.axis_index("ay")

        def others(v):
            doubled = jnp.concatenate([v, v], axis=0)
            return lax.dynamic_slice_in_dim(doubled, (z + 1) * nloc, (n_az - 1) * nloc, axis=0)

        first = lax.dynamic_slice_in_dim(b_rows, order[0] * rw, rw, axis=1)
        mine = [lax.all_gather(first, "az", axis=0, tiled=True)]
        theirs_own = swap(b_rows, "ay")
        w_own = row_weights(pair_index, e_occ, e_vir, occ_batch, freq)
        scaled_rows = lax.all_to_all(scale(w_own, b_rows), ("az", "ay"), 1, 0, tiled=True)
        theirs_own, rest = lax.optimization_barrier((theirs_own, b_rows))
        def x_chain(theirs):
            by_source = scaled_rows.reshape(n_az, n_ay, nloc, width)
            s_mine = lax.dynamic_index_in_dim(by_source, y, axis=1, keepdims=False).reshape(n_az * nloc, width)
            s_other = lax.dynamic_index_in_dim(by_source, 1 - y, axis=1, keepdims=False).reshape(n_az * nloc, width)
            s_a = lax.dynamic_slice_in_dim(s_other, z * nloc, nloc, axis=0)
            s_b = others(s_other)
            early = []
            for k, m in enumerate(order):
                cols_a = lax.dynamic_slice_in_dim(theirs_own, m * rw, rw, axis=1)
                early.append(contract(s_a, cols_a) + contract(s_mine, mine[k]))
            halves = 4 if width % 32 == 0 else 1
            hw = width // halves
            cuts = [slice(h * hw, (h + 1) * hw) for h in range(halves)]
            sent, got_x = [], []
            for rows in cuts:
                s_h = s_b[:, rows]
                give = early[0][rows] + contract(s_h, theirs[0])
                got = swap(give.astype(jnp.bfloat16), "rc").astype(jnp.float32)
                other_x = early[1][rows] + contract(s_h, theirs[1]) + got
                sent.append(other_x.astype(jnp.bfloat16))
                got_x.append(swap(sent[-1], "rx"))
            return s_a, s_b, early, tuple(sent), tuple(got_x), cuts, hw, halves

        x_out = {}
        theirs = [swap(others(mine[0]), "ay")]
        for m in order[1:]:
            _, _, rest = lax.optimization_barrier((mine[-1], theirs[-2] if len(theirs) > 1 else theirs_own, rest))
            piece = lax.all_gather(lax.dynamic_slice_in_dim(rest, m * rw, rw, axis=1), "az", axis=0, tiled=True)
            mine.append(piece)
            outgoing = others(piece)
            if len(mine) == len(order):
                x_out["v"] = x_chain(theirs)
                outgoing = lax.optimization_barrier((outgoing, x_out["v"][4]))[0]
            theirs.append(swap(outgoing, "ay"))
        s_a, s_b, early_part, sent, got_x, cuts, hw, halves = x_out["v"]
        early = list(early_part)
        _, late_give, t_give = lax.optimization_barrier((tuple(sent), early[2], theirs[2]))
        late_keep, t_keep = early[3], theirs[3]
        out = jnp.zeros((width, rw), jnp.float32)
        for h, rows in enumerate(cuts):
            s_h = s_b[:, rows]
            give = late_give[rows] + contract(s_h, t_give)
            own_x = late_keep[rows] + contract(s_h, t_keep) + swap(give, "rc")
            out = lax.dynamic_update_slice_in_dim(out, own_x + got_x[h].astype(jnp.float32), h * hw, axis=0)
            if h < halves - 1:
                out = lax.optimization_barrier(out)
        return out

    return body


def make_plain_body(n_rows, n_aux):
    def body(b_rows, pair_index, e_occ, e_vir, occ_batch, freq):
        width = b_rows.shape[1] // n_aux
        group_pairs = lax.all_gather(pair_index, "aux", axis=0, tiled=True)
        group = lax.all_gather(b_rows, "aux", axis=0, tiled=True)
        own = lax.dynamic_slice_in_dim(group, lax.axis_index("aux") * width, width, axis=1)
        scaled = scale(row_weights(group_pairs, e_occ, e_vir, occ_batch, freq), own)
        return lax.psum_scatter(contract(scaled, group), "rows", scatter_dimension=1, tiled=True)

    return body


def solution(mesh):
    n_rows = mesh.shape["rows"]
    n_aux = mesh.shape["aux"]
    naux = 8192
    fits = n_rows == 4 and n_aux % 2 == 0 and (naux // n_rows) % (naux // n_aux) == 0
    if not fits:
        placed = (P(("rows", "aux"), None), P(("rows", "aux")), P(), P(), P(), P())
        return jax.shard_map(
            make_plain_body(n_rows, n_aux), mesh=mesh, in_specs=placed,
            out_specs=P("aux", "rows"), check_vma=False,
        )
    n_rx, n_rc, n_ay = 2, 2, 2
    n_az = n_aux // n_ay
    split = Mesh(mesh.devices.reshape(n_rx, n_rc, n_az, n_ay), ("rx", "rc", "az", "ay"))
    rows_all = ("rx", "rc", "az", "ay")
    placed = (P(rows_all, None), P(rows_all), P(), P(), P(), P())
    return jax.shard_map(
        make_body(n_rx, n_rc, n_az, n_ay),
        mesh=split,
        in_specs=placed,
        out_specs=P(("az", "ay"), ("rx", "rc")),
        check_vma=False,
    )
```

```python
import jax
import jax.numpy as jnp
from jax import lax
from jax.sharding import Mesh, PartitionSpec as P

NVIR = 1536
NOCC_B = 4


def row_weights(pairs, e_occ, e_vir, occ_batch, freq):
    batch_start = occ_batch[0] * NOCC_B
    e_batch = lax.dynamic_slice_in_dim(e_occ, batch_start, NOCC_B, 0)
    occ = pairs // NVIR
    vir = pairs % NVIR
    occ_hit = occ[:, None] == jnp.arange(NOCC_B, dtype=jnp.int32)[None, :]
    vir_hit = vir[:, None] == jnp.arange(e_vir.shape[0], dtype=jnp.int32)[None, :]
    e_low = jnp.sum(jnp.where(occ_hit, e_batch[None, :], 0.0), axis=1)
    e_high = jnp.sum(jnp.where(vir_hit, e_vir[None, :], 0.0), axis=1)
    delta = e_high - e_low
    return 2.0 * delta / (delta * delta + freq[0] * freq[0])


def contract(left, right):
    return lax.dot_general(
        left, right, (((0,), (0,)), ((), ())), preferred_element_type=jnp.float32
    )


def swap(x, axis):
    return lax.ppermute(x, axis, [(0, 1), (1, 0)])


def scale(weight, cols):
    return (weight[:, None] * cols.astype(jnp.float32)).astype(jnp.bfloat16)


def make_body(n_rx, n_rc, n_az, n_ay):
    def body(b_rows, pair_index, e_occ, e_vir, occ_batch, freq):
        nloc, naux = b_rows.shape
        width = naux // (n_az * n_ay)
        rw = naux // (n_rx * n_rc)
        z = lax.axis_index("az")
        x = lax.axis_index("rx")
        c = lax.axis_index("rc")
        a = z * n_ay + lax.axis_index("ay")
        order = [(1 - x) * 2 + (1 - c), (1 - x) * 2 + c, x * 2 + (1 - c), x * 2 + c]
        y = lax.axis_index("ay")

        def others(v):
            doubled = jnp.concatenate([v, v], axis=0)
            return lax.dynamic_slice_in_dim(doubled, (z + 1) * nloc, (n_az - 1) * nloc, axis=0)

        first = lax.dynamic_slice_in_dim(b_rows, order[0] * rw, rw, axis=1)
        mine = [lax.all_gather(first, "az", axis=0, tiled=True)]
        theirs_own = swap(b_rows, "ay")
        w_own = row_weights(pair_index, e_occ, e_vir, occ_batch, freq)
        scaled_rows = lax.all_to_all(scale(w_own, b_rows), ("az", "ay"), 1, 0, tiled=True)
        theirs_own, rest = lax.optimization_barrier((theirs_own, b_rows))
        def x_chain(theirs):
            by_source = scaled_rows.reshape(n_az, n_ay, nloc, width)
            s_mine = lax.dynamic_index_in_dim(by_source, y, axis=1, keepdims=False).reshape(n_az * nloc, width)
            s_other = lax.dynamic_index_in_dim(by_source, 1 - y, axis=1, keepdims=False).reshape(n_az * nloc, width)
            s_a = lax.dynamic_slice_in_dim(s_other, z * nloc, nloc, axis=0)
            s_b = others(s_other)
            early = []
            for k, m in enumerate(order):
                cols_a = lax.dynamic_slice_in_dim(theirs_own, m * rw, rw, axis=1)
                early.append(contract(s_a, cols_a) + contract(s_mine, mine[k]))
            halves = 4 if width % 32 == 0 else 1
            hw = width // halves
            cuts = [slice(h * hw, (h + 1) * hw) for h in range(halves)]
            sent, got_x = [], []
            for rows in cuts:
                s_h = s_b[:, rows]
                give = early[0][rows] + contract(s_h, theirs[0])
                got = swap(give.astype(jnp.bfloat16), "rc").astype(jnp.float32)
                other_x = early[1][rows] + contract(s_h, theirs[1]) + got
                sent.append(other_x.astype(jnp.bfloat16))
                got_x.append(swap(sent[-1], "rx"))
            return s_a, s_b, early, tuple(sent), tuple(got_x), cuts, hw, halves

        x_out = {}
        theirs = [swap(others(mine[0]), "ay")]
        for m in order[1:]:
            _, _, rest = lax.optimization_barrier((mine[-1], theirs[-2] if len(theirs) > 1 else theirs_own, rest))
            piece = lax.all_gather(lax.dynamic_slice_in_dim(rest, m * rw, rw, axis=1), "az", axis=0, tiled=True)
            mine.append(piece)
            outgoing = others(piece)
            if len(mine) == len(order):
                x_out["v"] = x_chain(theirs)
                outgoing = lax.optimization_barrier((outgoing, x_out["v"][4][:-1] or x_out["v"][4]))[0]
            theirs.append(swap(outgoing, "ay"))
        s_a, s_b, early_part, sent, got_x, cuts, hw, halves = x_out["v"]
        early = list(early_part)
        _, _, late_give, t_give = lax.optimization_barrier((tuple(sent), got_x[-1], early[2], theirs[2]))
        late_keep, t_keep = early[3], theirs[3]
        out = jnp.zeros((width, rw), jnp.float32)
        for h, rows in enumerate(cuts):
            s_h = s_b[:, rows]
            give = late_give[rows] + contract(s_h, t_give)
            own_x = late_keep[rows] + contract(s_h, t_keep) + swap(give, "rc")
            out = lax.dynamic_update_slice_in_dim(out, own_x + got_x[h].astype(jnp.float32), h * hw, axis=0)
            if h < halves - 1:
                out = lax.optimization_barrier(out)
        return out

    return body


def make_plain_body(n_rows, n_aux):
    def body(b_rows, pair_index, e_occ, e_vir, occ_batch, freq):
        width = b_rows.shape[1] // n_aux
        group_pairs = lax.all_gather(pair_index, "aux", axis=0, tiled=True)
        group = lax.all_gather(b_rows, "aux", axis=0, tiled=True)
        own = lax.dynamic_slice_in_dim(group, lax.axis_index("aux") * width, width, axis=1)
        scaled = scale(row_weights(group_pairs, e_occ, e_vir, occ_batch, freq), own)
        return lax.psum_scatter(contract(scaled, group), "rows", scatter_dimension=1, tiled=True)

    return body


def solution(mesh):
    n_rows = mesh.shape["rows"]
    n_aux = mesh.shape["aux"]
    naux = 8192
    fits = n_rows == 4 and n_aux % 2 == 0 and (naux // n_rows) % (naux // n_aux) == 0
    if not fits:
        placed = (P(("rows", "aux"), None), P(("rows", "aux")), P(), P(), P(), P())
        return jax.shard_map(
            make_plain_body(n_rows, n_aux), mesh=mesh, in_specs=placed,
            out_specs=P("aux", "rows"), check_vma=False,
        )
    n_rx, n_rc, n_ay = 2, 2, 2
    n_az = n_aux // n_ay
    split = Mesh(mesh.devices.reshape(n_rx, n_rc, n_az, n_ay), ("rx", "rc", "az", "ay"))
    rows_all = ("rx", "rc", "az", "ay")
    placed = (P(rows_all, None), P(rows_all), P(), P(), P(), P())
    return jax.shard_map(
        make_body(n_rx, n_rc, n_az, n_ay),
        mesh=split,
        in_specs=placed,
        out_specs=P(("az", "ay"), ("rx", "rc")),
        check_vma=False,
    )
```

```python
import jax
import jax.numpy as jnp
from jax import lax
from jax.sharding import Mesh, PartitionSpec as P

NVIR = 1536
NOCC_B = 4


def row_weights(pairs, e_occ, e_vir, occ_batch, freq):
    batch_start = occ_batch[0] * NOCC_B
    e_batch = lax.dynamic_slice_in_dim(e_occ, batch_start, NOCC_B, 0)
    occ = pairs // NVIR
    vir = pairs % NVIR
    occ_hit = occ[:, None] == jnp.arange(NOCC_B, dtype=jnp.int32)[None, :]
    vir_hit = vir[:, None] == jnp.arange(e_vir.shape[0], dtype=jnp.int32)[None, :]
    e_low = jnp.sum(jnp.where(occ_hit, e_batch[None, :], 0.0), axis=1)
    e_high = jnp.sum(jnp.where(vir_hit, e_vir[None, :], 0.0), axis=1)
    delta = e_high - e_low
    return 2.0 * delta / (delta * delta + freq[0] * freq[0])


def contract(left, right):
    return lax.dot_general(
        left, right, (((0,), (0,)), ((), ())), preferred_element_type=jnp.float32
    )


def swap(x, axis):
    return lax.ppermute(x, axis, [(0, 1), (1, 0)])


def scale(weight, cols):
    return (weight[:, None] * cols.astype(jnp.float32)).astype(jnp.bfloat16)


def make_body(n_rx, n_rc, n_az, n_ay):
    def body(b_rows, pair_index, e_occ, e_vir, occ_batch, freq):
        nloc, naux = b_rows.shape
        width = naux // (n_az * n_ay)
        rw = naux // (n_rx * n_rc)
        z = lax.axis_index("az")
        x = lax.axis_index("rx")
        c = lax.axis_index("rc")
        a = z * n_ay + lax.axis_index("ay")
        order = [(1 - x) * 2 + (1 - c), (1 - x) * 2 + c, x * 2 + (1 - c), x * 2 + c]
        y = lax.axis_index("ay")

        def others(v):
            doubled = jnp.concatenate([v, v], axis=0)
            return lax.dynamic_slice_in_dim(doubled, (z + 1) * nloc, (n_az - 1) * nloc, axis=0)

        first = lax.dynamic_slice_in_dim(b_rows, order[0] * rw, rw, axis=1)
        mine = [lax.all_gather(first, "az", axis=0, tiled=True)]
        theirs_own = swap(b_rows, "ay")
        w_own = row_weights(pair_index, e_occ, e_vir, occ_batch, freq)
        scaled_rows = lax.all_to_all(scale(w_own, b_rows), ("az", "ay"), 1, 0, tiled=True)
        theirs_own, rest = lax.optimization_barrier((theirs_own, b_rows))
        def x_chain(theirs):
            by_source = scaled_rows.reshape(n_az, n_ay, nloc, width)
            s_mine = lax.dynamic_index_in_dim(by_source, y, axis=1, keepdims=False).reshape(n_az * nloc, width)
            s_other = lax.dynamic_index_in_dim(by_source, 1 - y, axis=1, keepdims=False).reshape(n_az * nloc, width)
            s_a = lax.dynamic_slice_in_dim(s_other, z * nloc, nloc, axis=0)
            s_b = others(s_other)
            early = []
            for k, m in enumerate(order):
                cols_a = lax.dynamic_slice_in_dim(theirs_own, m * rw, rw, axis=1)
                early.append(contract(s_a, cols_a) + contract(s_mine, mine[k]))
            halves = 4 if width % 32 == 0 else 1
            hw = width // halves
            cuts = [slice(h * hw, (h + 1) * hw) for h in range(halves)]
            sent, got_x = [], []
            for rows in cuts:
                s_h = s_b[:, rows]
                give = early[0][rows] + contract(s_h, theirs[0])
                got = swap(give.astype(jnp.bfloat16), "rc").astype(jnp.float32)
                other_x = early[1][rows] + contract(s_h, theirs[1]) + got
                sent.append(other_x.astype(jnp.bfloat16))
                got_x.append(swap(sent[-1], "rx"))
            return s_a, s_b, early, tuple(sent), tuple(got_x), cuts, hw, halves

        x_out = {}
        theirs = [swap(others(mine[0]), "ay")]
        for m in order[1:]:
            _, _, rest = lax.optimization_barrier((mine[-1], theirs[-2] if len(theirs) > 1 else theirs_own, rest))
            piece = lax.all_gather(lax.dynamic_slice_in_dim(rest, m * rw, rw, axis=1), "az", axis=0, tiled=True)
            mine.append(piece)
            outgoing = others(piece)
            if len(mine) == len(order):
                x_out["v"] = x_chain(theirs)
                outgoing = lax.optimization_barrier((outgoing, x_out["v"][4][:2]))[0]
            theirs.append(swap(outgoing, "ay"))
        s_a, s_b, early_part, sent, got_x, cuts, hw, halves = x_out["v"]
        early = list(early_part)
        _, _, late_give, t_give = lax.optimization_barrier((tuple(sent), got_x[2:], early[2], theirs[2]))
        late_keep, t_keep = early[3], theirs[3]
        out = jnp.zeros((width, rw), jnp.float32)
        for h, rows in enumerate(cuts):
            s_h = s_b[:, rows]
            give = late_give[rows] + contract(s_h, t_give)
            own_x = late_keep[rows] + contract(s_h, t_keep) + swap(give, "rc")
            out = lax.dynamic_update_slice_in_dim(out, own_x + got_x[h].astype(jnp.float32), h * hw, axis=0)
            if h < halves - 1:
                out = lax.optimization_barrier(out)
        return out

    return body


def make_plain_body(n_rows, n_aux):
    def body(b_rows, pair_index, e_occ, e_vir, occ_batch, freq):
        width = b_rows.shape[1] // n_aux
        group_pairs = lax.all_gather(pair_index, "aux", axis=0, tiled=True)
        group = lax.all_gather(b_rows, "aux", axis=0, tiled=True)
        own = lax.dynamic_slice_in_dim(group, lax.axis_index("aux") * width, width, axis=1)
        scaled = scale(row_weights(group_pairs, e_occ, e_vir, occ_batch, freq), own)
        return lax.psum_scatter(contract(scaled, group), "rows", scatter_dimension=1, tiled=True)

    return body


def solution(mesh):
    n_rows = mesh.shape["rows"]
    n_aux = mesh.shape["aux"]
    naux = 8192
    fits = n_rows == 4 and n_aux % 2 == 0 and (naux // n_rows) % (naux // n_aux) == 0
    if not fits:
        placed = (P(("rows", "aux"), None), P(("rows", "aux")), P(), P(), P(), P())
        return jax.shard_map(
            make_plain_body(n_rows, n_aux), mesh=mesh, in_specs=placed,
            out_specs=P("aux", "rows"), check_vma=False,
        )
    n_rx, n_rc, n_ay = 2, 2, 2
    n_az = n_aux // n_ay
    split = Mesh(mesh.devices.reshape(n_rx, n_rc, n_az, n_ay), ("rx", "rc", "az", "ay"))
    rows_all = ("rx", "rc", "az", "ay")
    placed = (P(rows_all, None), P(rows_all), P(), P(), P(), P())
    return jax.shard_map(
        make_body(n_rx, n_rc, n_az, n_ay),
        mesh=split,
        in_specs=placed,
        out_specs=P(("az", "ay"), ("rx", "rc")),
        check_vma=False,
    )
```

```python
import jax
import jax.numpy as jnp
from jax import lax
from jax.sharding import Mesh, PartitionSpec as P

NVIR = 1536
NOCC_B = 4


def row_weights(pairs, e_occ, e_vir, occ_batch, freq):
    batch_start = occ_batch[0] * NOCC_B
    e_batch = lax.dynamic_slice_in_dim(e_occ, batch_start, NOCC_B, 0)
    occ = pairs // NVIR
    vir = pairs % NVIR
    occ_hit = occ[:, None] == jnp.arange(NOCC_B, dtype=jnp.int32)[None, :]
    vir_hit = vir[:, None] == jnp.arange(e_vir.shape[0], dtype=jnp.int32)[None, :]
    e_low = jnp.sum(jnp.where(occ_hit, e_batch[None, :], 0.0), axis=1)
    e_high = jnp.sum(jnp.where(vir_hit, e_vir[None, :], 0.0), axis=1)
    delta = e_high - e_low
    return 2.0 * delta / (delta * delta + freq[0] * freq[0])


def contract(left, right):
    return lax.dot_general(
        left, right, (((0,), (0,)), ((), ())), preferred_element_type=jnp.float32
    )


def swap(x, axis):
    return lax.ppermute(x, axis, [(0, 1), (1, 0)])


def scale(weight, cols):
    return (weight[:, None] * cols.astype(jnp.float32)).astype(jnp.bfloat16)


def make_body(n_rx, n_rc, n_az, n_ay):
    def body(b_rows, pair_index, e_occ, e_vir, occ_batch, freq):
        nloc, naux = b_rows.shape
        width = naux // (n_az * n_ay)
        rw = naux // (n_rx * n_rc)
        z = lax.axis_index("az")
        x = lax.axis_index("rx")
        c = lax.axis_index("rc")
        a = z * n_ay + lax.axis_index("ay")
        order = [(1 - x) * 2 + (1 - c), (1 - x) * 2 + c, x * 2 + (1 - c), x * 2 + c]
        y = lax.axis_index("ay")

        def others(v):
            doubled = jnp.concatenate([v, v], axis=0)
            return lax.dynamic_slice_in_dim(doubled, (z + 1) * nloc, (n_az - 1) * nloc, axis=0)

        first = lax.dynamic_slice_in_dim(b_rows, order[0] * rw, rw, axis=1)
        mine = [lax.all_gather(first, "az", axis=0, tiled=True)]
        theirs_own = swap(b_rows, "ay")
        w_own = row_weights(pair_index, e_occ, e_vir, occ_batch, freq)
        scaled_rows = lax.all_to_all(scale(w_own, b_rows), ("az", "ay"), 1, 0, tiled=True)
        theirs_own, rest = lax.optimization_barrier((theirs_own, b_rows))
        def x_chain(theirs):
            by_source = scaled_rows.reshape(n_az, n_ay, nloc, width)
            s_mine = lax.dynamic_index_in_dim(by_source, y, axis=1, keepdims=False).reshape(n_az * nloc, width)
            s_other = lax.dynamic_index_in_dim(by_source, 1 - y, axis=1, keepdims=False).reshape(n_az * nloc, width)
            s_a = lax.dynamic_slice_in_dim(s_other, z * nloc, nloc, axis=0)
            s_b = others(s_other)
            early = []
            for k, m in enumerate(order):
                cols_a = lax.dynamic_slice_in_dim(theirs_own, m * rw, rw, axis=1)
                early.append(contract(s_a, cols_a) + contract(s_mine, mine[k]))
            halves = 4 if width % 32 == 0 else 1
            hw = width // halves
            cuts = [slice(h * hw, (h + 1) * hw) for h in range(halves)]
            sent, got_x = [], []
            for rows in cuts:
                s_h = s_b[:, rows]
                give = early[0][rows] + contract(s_h, theirs[0])
                got = swap(give.astype(jnp.bfloat16), "rc").astype(jnp.float32)
                other_x = early[1][rows] + contract(s_h, theirs[1]) + got
                sent.append(other_x.astype(jnp.bfloat16))
                got_x.append(swap(sent[-1], "rx"))
            return s_a, s_b, early, tuple(sent), tuple(got_x), cuts, hw, halves

        x_out = {}
        theirs = [swap(others(mine[0]), "ay")]
        for m in order[1:]:
            _, _, rest = lax.optimization_barrier((mine[-1], theirs[-2] if len(theirs) > 1 else theirs_own, rest))
            piece = lax.all_gather(lax.dynamic_slice_in_dim(rest, m * rw, rw, axis=1), "az", axis=0, tiled=True)
            mine.append(piece)
            outgoing = others(piece)
            if len(mine) == len(order):
                x_out["v"] = x_chain(theirs)
                outgoing = lax.optimization_barrier((outgoing, x_out["v"][3]))[0]
            theirs.append(swap(outgoing, "ay"))
        s_a, s_b, early_part, sent, got_x, cuts, hw, halves = x_out["v"]
        early = list(early_part)
        _, _, late_give, t_give = lax.optimization_barrier((tuple(sent), got_x, early[2], theirs[2]))
        late_keep, t_keep = early[3], theirs[3]
        out = jnp.zeros((width, rw), jnp.float32)
        for h, rows in enumerate(cuts):
            s_h = s_b[:, rows]
            give = late_give[rows] + contract(s_h, t_give)
            own_x = late_keep[rows] + contract(s_h, t_keep) + swap(give, "rc")
            out = lax.dynamic_update_slice_in_dim(out, own_x + got_x[h].astype(jnp.float32), h * hw, axis=0)
            if h < halves - 1:
                out = lax.optimization_barrier(out)
        return out

    return body


def make_plain_body(n_rows, n_aux):
    def body(b_rows, pair_index, e_occ, e_vir, occ_batch, freq):
        width = b_rows.shape[1] // n_aux
        group_pairs = lax.all_gather(pair_index, "aux", axis=0, tiled=True)
        group = lax.all_gather(b_rows, "aux", axis=0, tiled=True)
        own = lax.dynamic_slice_in_dim(group, lax.axis_index("aux") * width, width, axis=1)
        scaled = scale(row_weights(group_pairs, e_occ, e_vir, occ_batch, freq), own)
        return lax.psum_scatter(contract(scaled, group), "rows", scatter_dimension=1, tiled=True)

    return body


def solution(mesh):
    n_rows = mesh.shape["rows"]
    n_aux = mesh.shape["aux"]
    naux = 8192
    fits = n_rows == 4 and n_aux % 2 == 0 and (naux // n_rows) % (naux // n_aux) == 0
    if not fits:
        placed = (P(("rows", "aux"), None), P(("rows", "aux")), P(), P(), P(), P())
        return jax.shard_map(
            make_plain_body(n_rows, n_aux), mesh=mesh, in_specs=placed,
            out_specs=P("aux", "rows"), check_vma=False,
        )
    n_rx, n_rc, n_ay = 2, 2, 2
    n_az = n_aux // n_ay
    split = Mesh(mesh.devices.reshape(n_rx, n_rc, n_az, n_ay), ("rx", "rc", "az", "ay"))
    rows_all = ("rx", "rc", "az", "ay")
    placed = (P(rows_all, None), P(rows_all), P(), P(), P(), P())
    return jax.shard_map(
        make_body(n_rx, n_rc, n_az, n_ay),
        mesh=split,
        in_specs=placed,
        out_specs=P(("az", "ay"), ("rx", "rc")),
        check_vma=False,
    )
```

```python
import jax
import jax.numpy as jnp
from jax import lax
from jax.sharding import Mesh, PartitionSpec as P

NVIR = 1536
NOCC_B = 4


def row_weights(pairs, e_occ, e_vir, occ_batch, freq):
    batch_start = occ_batch[0] * NOCC_B
    e_batch = lax.dynamic_slice_in_dim(e_occ, batch_start, NOCC_B, 0)
    occ = pairs // NVIR
    vir = pairs % NVIR
    occ_hit = occ[:, None] == jnp.arange(NOCC_B, dtype=jnp.int32)[None, :]
    vir_hit = vir[:, None] == jnp.arange(e_vir.shape[0], dtype=jnp.int32)[None, :]
    e_low = jnp.sum(jnp.where(occ_hit, e_batch[None, :], 0.0), axis=1)
    e_high = jnp.sum(jnp.where(vir_hit, e_vir[None, :], 0.0), axis=1)
    delta = e_high - e_low
    return 2.0 * delta / (delta * delta + freq[0] * freq[0])


def contract(left, right):
    return lax.dot_general(
        left, right, (((0,), (0,)), ((), ())), preferred_element_type=jnp.float32
    )


def swap(x, axis):
    return lax.ppermute(x, axis, [(0, 1), (1, 0)])


def scale(weight, cols):
    return (weight[:, None] * cols.astype(jnp.float32)).astype(jnp.bfloat16)


def make_body(n_rx, n_rc, n_az, n_ay):
    def body(b_rows, pair_index, e_occ, e_vir, occ_batch, freq):
        nloc, naux = b_rows.shape
        width = naux // (n_az * n_ay)
        rw = naux // (n_rx * n_rc)
        z = lax.axis_index("az")
        x = lax.axis_index("rx")
        c = lax.axis_index("rc")
        a = z * n_ay + lax.axis_index("ay")
        order = [(1 - x) * 2 + (1 - c), (1 - x) * 2 + c, x * 2 + (1 - c), x * 2 + c]
        y = lax.axis_index("ay")

        def others(v):
            doubled = jnp.concatenate([v, v], axis=0)
            return lax.dynamic_slice_in_dim(doubled, (z + 1) * nloc, (n_az - 1) * nloc, axis=0)

        first = lax.dynamic_slice_in_dim(b_rows, order[0] * rw, rw, axis=1)
        mine = [lax.all_gather(first, "az", axis=0, tiled=True)]
        theirs_own = swap(b_rows, "ay")
        w_own = row_weights(pair_index, e_occ, e_vir, occ_batch, freq)
        scaled_rows = lax.all_to_all(scale(w_own, b_rows), ("az", "ay"), 1, 0, tiled=True)
        theirs_own, rest = lax.optimization_barrier((theirs_own, b_rows))
        def x_chain(theirs):
            by_source = scaled_rows.reshape(n_az, n_ay, nloc, width)
            s_mine = lax.dynamic_index_in_dim(by_source, y, axis=1, keepdims=False).reshape(n_az * nloc, width)
            s_other = lax.dynamic_index_in_dim(by_source, 1 - y, axis=1, keepdims=False).reshape(n_az * nloc, width)
            s_a = lax.dynamic_slice_in_dim(s_other, z * nloc, nloc, axis=0)
            s_b = others(s_other)
            early = []
            for k, m in enumerate(order):
                cols_a = lax.dynamic_slice_in_dim(theirs_own, m * rw, rw, axis=1)
                early.append(contract(s_a, cols_a) + contract(s_mine, mine[k]))
            halves = 4 if width % 32 == 0 else 1
            hw = width // halves
            cuts = [slice(h * hw, (h + 1) * hw) for h in range(halves)]
            sent, got_x = [], []
            for rows in cuts:
                s_h = s_b[:, rows]
                give = early[0][rows] + contract(s_h, theirs[0])
                got = swap(give.astype(jnp.bfloat16), "rc").astype(jnp.float32)
                other_x = early[1][rows] + contract(s_h, theirs[1]) + got
                sent.append(other_x.astype(jnp.bfloat16))
                got_x.append(swap(sent[-1], "rx"))
            return s_a, s_b, early, tuple(sent), tuple(got_x), cuts, hw, halves

        x_out = {}
        theirs = [swap(others(mine[0]), "ay")]
        for m in order[1:]:
            _, _, rest = lax.optimization_barrier((mine[-1], theirs[-2] if len(theirs) > 1 else theirs_own, rest))
            piece = lax.all_gather(lax.dynamic_slice_in_dim(rest, m * rw, rw, axis=1), "az", axis=0, tiled=True)
            mine.append(piece)
            outgoing = others(piece)
            if len(mine) == len(order):
                x_out["v"] = x_chain(theirs)
                outgoing = lax.optimization_barrier((outgoing, x_out["v"][4][:1]))[0]
            theirs.append(swap(outgoing, "ay"))
        s_a, s_b, early_part, sent, got_x, cuts, hw, halves = x_out["v"]
        early = list(early_part)
        _, _, late_give, t_give = lax.optimization_barrier((tuple(sent), got_x[1:], early[2], theirs[2]))
        late_keep, t_keep = early[3], theirs[3]
        out = jnp.zeros((width, rw), jnp.float32)
        for h, rows in enumerate(cuts):
            s_h = s_b[:, rows]
            give = late_give[rows] + contract(s_h, t_give)
            own_x = late_keep[rows] + contract(s_h, t_keep) + swap(give, "rc")
            out = lax.dynamic_update_slice_in_dim(out, own_x + got_x[h].astype(jnp.float32), h * hw, axis=0)
            if h < halves - 1:
                out = lax.optimization_barrier(out)
        return out

    return body


def make_plain_body(n_rows, n_aux):
    def body(b_rows, pair_index, e_occ, e_vir, occ_batch, freq):
        width = b_rows.shape[1] // n_aux
        group_pairs = lax.all_gather(pair_index, "aux", axis=0, tiled=True)
        group = lax.all_gather(b_rows, "aux", axis=0, tiled=True)
        own = lax.dynamic_slice_in_dim(group, lax.axis_index("aux") * width, width, axis=1)
        scaled = scale(row_weights(group_pairs, e_occ, e_vir, occ_batch, freq), own)
        return lax.psum_scatter(contract(scaled, group), "rows", scatter_dimension=1, tiled=True)

    return body


def solution(mesh):
    n_rows = mesh.shape["rows"]
    n_aux = mesh.shape["aux"]
    naux = 8192
    fits = n_rows == 4 and n_aux % 2 == 0 and (naux // n_rows) % (naux // n_aux) == 0
    if not fits:
        placed = (P(("rows", "aux"), None), P(("rows", "aux")), P(), P(), P(), P())
        return jax.shard_map(
            make_plain_body(n_rows, n_aux), mesh=mesh, in_specs=placed,
            out_specs=P("aux", "rows"), check_vma=False,
        )
    n_rx, n_rc, n_ay = 2, 2, 2
    n_az = n_aux // n_ay
    split = Mesh(mesh.devices.reshape(n_rx, n_rc, n_az, n_ay), ("rx", "rc", "az", "ay"))
    rows_all = ("rx", "rc", "az", "ay")
    placed = (P(rows_all, None), P(rows_all), P(), P(), P(), P())
    return jax.shard_map(
        make_body(n_rx, n_rc, n_az, n_ay),
        mesh=split,
        in_specs=placed,
        out_specs=P(("az", "ay"), ("rx", "rc")),
        check_vma=False,
    )
```
